256 devices in a mesh: lon: 64 (over x_hi, z, y), lat: 4 (over x_lo, core).
Axes of the slice: x: 4 (x_hi: 2, x_lo: 2; x = x_hi * 2 + x_lo), y: 4, z: 8, core: 2. Of those that a mesh axis runs over, the one named last changes fastest.
Arguments:
- thermal_anomaly: float32 [25, 64, 65536], P(None, 'lat', 'lon'), may hold values from -6 to 6
- saltiness_anomaly: float32 [25, 64, 65536], P(None, 'lat', 'lon'), may hold values from -6 to 6
- zonal_velocity_array: float32 [25, 64, 65536], P(None, 'lat', 'lon'), may hold values from -6 to 6
- meridional_velocity_array: float32 [25, 64, 65536], P(None, 'lat', 'lon'), may hold values from -6 to 6
- seawater_profile_flags: int32 [64, 65536], P('lat', 'lon'), may hold values 0 or 1
- submerged_layer_total: int32 [64, 65536], P('lat', 'lon'), may hold values from 0 to 25
- computed_block_flags: int32 [4, 64], P('lat', 'lon'), may hold values 0 or 1
Outputs:
- next_temperature: float32 [25, 64, 65536], P(None, 'lat', 'lon')
- next_salinity: float32 [25, 64, 65536], P(None, 'lat', 'lon')
- next_zonal: float32 [25, 64, 65536], P(None, 'lat', 'lon')
- next_meridional: float32 [25, 64, 65536], P(None, 'lat', 'lon')
The draws below stay inside these ranges and needn't reach their ends.
All inputs are finite; a program needn't handle non-finite values. No bound on the sum of `seawater_profile_flags` or of `computed_block_flags` on one device may be relied on, other than what follows from the above.
Results may differ from the reference program's by a relative error of at most 0.00002.
Values sent between devices are 32-bit elements; how exact they have to be, the bound alone decides.
No kernel may reach another device: no remote copies, remote signals or barrier semaphores. Data moves between devices by JAX's collectives and lax.ppermute only.
A program may use at most 192 MiB of HBM per device.

```python
import jax
import jax.numpy as jnp

DEPTH_LAYERS = 25
CX = 1024
CY = 16
ZONAL_SIZE = 65536
MERIDIONAL_SIZE = 64
TILES_LAT = 4
TILES_LON = 64


def plant(entries, key, low, high):
    place = [jax.random.randint(jax.random.fold_in(key, axis), (), 0, length) for axis, length in enumerate(entries.shape)]
    widest = entries.shape.index(max(entries.shape))
    neighbour = place[:widest] + [(place[widest] + 1) % entries.shape[widest]] + place[widest + 1:]
    return entries.at[tuple(place)].set(low).at[tuple(neighbour)].set(high)


def level_of(key, extent, pieces, smallest, top_value):
    def one(axis_at, parts):
        steps = jax.random.uniform(jax.random.fold_in(jax.random.fold_in(key, 6), axis_at), (parts,), jnp.float32, smallest / len(pieces), top_value / len(pieces))
        return jnp.repeat(jnp.exp(steps), extent[axis_at] // parts).reshape((-1,) + (1,) * (len(extent) - axis_at - 1))

    gain = one(*pieces[0])
    for cut in pieces[1:]:
        gain = gain * one(*cut)
    return gain


def normal_values(stream_key, extent, spread, reach, split=(), kind=jnp.bfloat16):
    result = spread * jax.random.normal(stream_key, extent, jnp.float32)
    if split:
        result = result * level_of(stream_key, extent, split, -0.22, 0.18)
    return jnp.clip(result, -reach, reach).astype(kind)


def setup_inputs(seed: int = 0) -> dict:
    arg_keys = jax.random.split(jax.random.key(seed), 8)
    return {
        "thermal_anomaly": normal_values(arg_keys[0], (DEPTH_LAYERS, MERIDIONAL_SIZE, ZONAL_SIZE), 1.0, 6.0, ((1, 4), (2, 64)), jnp.float32),
        "saltiness_anomaly": normal_values(arg_keys[1], (DEPTH_LAYERS, MERIDIONAL_SIZE, ZONAL_SIZE), 1.0, 6.0, ((1, 4), (2, 64)), jnp.float32),
        "zonal_velocity_array": normal_values(arg_keys[2], (DEPTH_LAYERS, MERIDIONAL_SIZE, ZONAL_SIZE), 1.0, 6.0, ((1, 4), (2, 64)), jnp.float32),
        "meridional_velocity_array": normal_values(arg_keys[3], (DEPTH_LAYERS, MERIDIONAL_SIZE, ZONAL_SIZE), 1.0, 6.0, ((1, 4), (2, 64)), jnp.float32),
        "seawater_profile_flags": plant((jax.random.randint(arg_keys[4], (MERIDIONAL_SIZE, ZONAL_SIZE), 0, 8) < 7).astype(jnp.int32), jax.random.fold_in(arg_keys[4], 1), 0, 1),
        "submerged_layer_total": plant(jax.random.randint(arg_keys[5], (MERIDIONAL_SIZE, ZONAL_SIZE), 0, DEPTH_LAYERS + 1), jax.random.fold_in(arg_keys[5], 1), 0, DEPTH_LAYERS).astype(jnp.int32),
        "computed_block_flags": plant((jax.random.randint(arg_keys[6], (TILES_LAT, TILES_LON), 0, 4) < 3).astype(jnp.int32), jax.random.fold_in(arg_keys[6], 1), 0, 1),
    }


ALPHA = 0.2
BETA = 0.8
GRAV_DZ = 0.1
DT_STEP = 0.2
VISC_TWO = 0.1
VISC_FOUR = 0.05
CORIOLIS_MAX = 0.3


def laplace(field):
    return (field[..., 2:, 1:-1] + field[..., :-2, 1:-1] + field[..., 1:-1, 2:]
            + field[..., 1:-1, :-2] - 4.0 * field[..., 1:-1, 1:-1])


def update_fields(extended, submerged_share, coriolis):
    temper = extended[0]
    saline = extended[1]
    eastward = extended[2]
    northward = extended[3]
    density = BETA * saline - ALPHA * temper
    pressure = GRAV_DZ * (jnp.cumsum(density, axis=0) - 0.5 * density)
    laplacian = laplace(extended)
    bilaplacian = laplace(laplacian)
    centre = extended[..., 2:-2, 2:-2]
    mixing = VISC_TWO * laplacian[..., 1:-1, 1:-1] - VISC_FOUR * bilaplacian
    grad_east = 0.5 * (pressure[:, 2:-2, 3:-1] - pressure[:, 2:-2, 1:-3])
    grad_north = 0.5 * (pressure[:, 3:-1, 2:-2] - pressure[:, 1:-3, 2:-2])
    tracers = extended[0:2]
    flux_east = tracers * eastward
    flux_north = tracers * northward
    advection = (0.5 * (flux_east[..., 2:-2, 3:-1] - flux_east[..., 2:-2, 1:-3])
                 + 0.5 * (flux_north[..., 3:-1, 2:-2] - flux_north[..., 1:-3, 2:-2]))
    accel_east = coriolis * centre[3] - grad_east
    accel_north = -coriolis * centre[2] - grad_north
    forcing = jnp.concatenate([-advection, accel_east[None], accel_north[None]], axis=0)
    return submerged_share * (centre + DT_STEP * (forcing + mixing))


def reference(thermal_anomaly, saltiness_anomaly, zonal_velocity_array, meridional_velocity_array, seawater_profile_flags, submerged_layer_total, computed_block_flags):
    tiles = jnp.repeat(jnp.repeat(computed_block_flags, CY, axis=0), CX, axis=1)
    depth_index = jnp.arange(DEPTH_LAYERS, dtype=jnp.int32)[:, None, None]
    submerged_share = ((depth_index < submerged_layer_total[None]) & (seawater_profile_flags[None] == 1)
               & (tiles[None] == 1)).astype(jnp.float32)
    evolving_state_arrays = jnp.stack([thermal_anomaly, saltiness_anomaly, zonal_velocity_array, meridional_velocity_array]) * submerged_share
    widened = jnp.concatenate([evolving_state_arrays[..., -2:], evolving_state_arrays, evolving_state_arrays[..., :2]], axis=3)
    signs = jnp.array([1.0, 1.0, -1.0, -1.0], jnp.float32).reshape(4, 1, 1, 1)
    northern = widened[:, :, -1:-3:-1, ::-1] * signs
    southern = jnp.zeros_like(northern)
    extended = jnp.concatenate([southern, widened, northern], axis=2)
    row_pos = jnp.arange(MERIDIONAL_SIZE, dtype=jnp.float32)
    coriolis = (CORIOLIS_MAX * jnp.sin(jnp.pi * ((row_pos + 0.5) / MERIDIONAL_SIZE - 0.5)))[:, None]
    updated = update_fields(extended, submerged_share, coriolis)
    return updated[0], updated[1], updated[2], updated[3]
```

```python
import jax
import jax.numpy as jnp
from jax import lax
from jax.sharding import PartitionSpec as P

ALPHA = 0.2
BETA = 0.8
GRAV_DZ = 0.1
DT_STEP = 0.2
VISC_TWO = 0.1
VISC_FOUR = 0.05
CORIOLIS_MAX = 0.3


def with_halo(value, sides, width, wrap):
    for axis, dim in sides:
        count, length = (lax.axis_size(axis), value.shape[dim])
        up = [(i, (i + 1) % count) for i in range(count if wrap else count - 1)]
        down = [(j, i) for i, j in up]
        last = lax.slice_in_dim(value, length - width, length, axis=dim)
        first = lax.slice_in_dim(value, 0, width, axis=dim)
        before = lax.ppermute(last, axis, up)
        after = lax.ppermute(first, axis, down)
        value = jnp.concatenate([before, value, after], axis=dim)
    return value


def from_partner(value, axis, distance):
    mask = 2**distance
    pairs = [(source, source ^ mask) for source in range(lax.axis_size(axis))]
    return lax.ppermute(value, axis, pairs)


def laplace(field):
    return (
        field[..., 2:, 1:-1]
        + field[..., :-2, 1:-1]
        + field[..., 1:-1, 2:]
        + field[..., 1:-1, :-2]
        - 4.0 * field[..., 1:-1, 1:-1]
    )


def update_fields(extended, submerged_share, coriolis):
    temper = extended[0]
    saline = extended[1]
    eastward = extended[2]
    northward = extended[3]
    density = BETA * saline - ALPHA * temper
    pressure = GRAV_DZ * (jnp.cumsum(density, axis=0) - 0.5 * density)
    laplacian = laplace(extended)
    bilaplacian = laplace(laplacian)
    centre = extended[..., 2:-2, 2:-2]
    mixing = VISC_TWO * laplacian[..., 1:-1, 1:-1] - VISC_FOUR * bilaplacian
    grad_east = 0.5 * (pressure[:, 2:-2, 3:-1] - pressure[:, 2:-2, 1:-3])
    grad_north = 0.5 * (pressure[:, 3:-1, 2:-2] - pressure[:, 1:-3, 2:-2])
    tracers = extended[0:2]
    flux_east = tracers * eastward
    flux_north = tracers * northward
    advection = 0.5 * (flux_east[..., 2:-2, 3:-1] - flux_east[..., 2:-2, 1:-3]) + 0.5 * (
        flux_north[..., 3:-1, 2:-2] - flux_north[..., 1:-3, 2:-2]
    )
    accel_east = coriolis * centre[3] - grad_east
    accel_north = -coriolis * centre[2] - grad_north
    forcing = jnp.concatenate([-advection, accel_east[None], accel_north[None]], axis=0)
    return submerged_share * (centre + DT_STEP * (forcing + mixing))


def shift_pairs(count, step, wrap):
    pairs = []
    for i in range(count):
        j = i + step
        if wrap:
            pairs.append((i, j % count))
        elif 0 <= j < count:
            pairs.append((i, j))
    return pairs


def per_device(
    thermal_anomaly,
    saltiness_anomaly,
    zonal_velocity_array,
    meridional_velocity_array,
    seawater_profile_flags,
    submerged_layer_total,
    computed_block_flags,
):
    block_depth_layers = thermal_anomaly.shape[0]
    block_meridional_extent = thermal_anomaly.shape[1]
    n_lon = lax.axis_size("lon")
    n_lat = lax.axis_size("lat")
    tile_alive = computed_block_flags[0, 0] == 1
    depth_index = jnp.arange(block_depth_layers, dtype=jnp.int32)[:, None, None]
    submerged_share = (
        (depth_index < submerged_layer_total[None])
        & (seawater_profile_flags[None] == 1)
        & tile_alive
    ).astype(jnp.float32)
    fields = (
        jnp.stack(
            [thermal_anomaly, saltiness_anomaly, zonal_velocity_array, meridional_velocity_array]
        )
        * submerged_share
    )
    top = fields[:, :, -2:, :]
    bottom = fields[:, :, :2, :]
    from_south = lax.ppermute(top, "lat", shift_pairs(n_lat, 1, False))
    from_north = lax.ppermute(bottom, "lat", shift_pairs(n_lat, -1, False))
    last = n_lat - 1
    fold_pairs = [(p * n_lat + last, (n_lon - 1 - p) * n_lat + last) for p in range(n_lon)]
    folded = lax.ppermute(top, ("lon", "lat"), fold_pairs)
    signs = jnp.array([1.0, 1.0, -1.0, -1.0], jnp.float32).reshape(4, 1, 1, 1)
    fold_rows = folded[:, :, ::-1, ::-1] * signs
    is_northern = lax.axis_index("lat") == last
    north = jnp.where(is_northern, fold_rows, from_north)
    tall = jnp.concatenate([from_south, fields, north], axis=2)
    west = lax.ppermute(tall[..., -2:], "lon", shift_pairs(n_lon, 1, True))
    east = lax.ppermute(tall[..., :2], "lon", shift_pairs(n_lon, -1, True))
    extended = jnp.concatenate([west, tall, east], axis=3)
    total_rows = block_meridional_extent * n_lat
    row_pos = (
        lax.axis_index("lat") * block_meridional_extent
        + jnp.arange(block_meridional_extent, dtype=jnp.int32)
    ).astype(jnp.float32)
    coriolis = (CORIOLIS_MAX * jnp.sin(jnp.pi * ((row_pos + 0.5) / total_rows - 0.5)))[:, None]
    updated = update_fields(extended, submerged_share, coriolis)
    return (updated[0], updated[1], updated[2], updated[3])


def solution(mesh):
    return jax.shard_map(
        per_device,
        mesh=mesh,
        in_specs=(
            P(None, "lat", "lon"),
            P(None, "lat", "lon"),
            P(None, "lat", "lon"),
            P(None, "lat", "lon"),
            P("lat", "lon"),
            P("lat", "lon"),
            P("lat", "lon"),
        ),
        out_specs=(
            P(None, "lat", "lon"),
            P(None, "lat", "lon"),
            P(None, "lat", "lon"),
            P(None, "lat", "lon"),
        ),
        check_vma=False,
    )
```

```python
import jax
import jax.numpy as jnp
from jax import lax
from jax.sharding import PartitionSpec as P
from jax.experimental import pallas as pl
from jax.experimental.pallas import tpu as pltpu

ALPHA = 0.2
BETA = 0.8
GRAV_DZ = 0.1
DT_STEP = 0.2
VISC_TWO = 0.1
VISC_FOUR = 0.05
CORIOLIS_MAX = 0.3


def with_halo(value, sides, width, wrap):
    for axis, dim in sides:
        count, length = (lax.axis_size(axis), value.shape[dim])
        up = [(i, (i + 1) % count) for i in range(count if wrap else count - 1)]
        down = [(j, i) for i, j in up]
        last = lax.slice_in_dim(value, length - width, length, axis=dim)
        first = lax.slice_in_dim(value, 0, width, axis=dim)
        before = lax.ppermute(last, axis, up)
        after = lax.ppermute(first, axis, down)
        value = jnp.concatenate([before, value, after], axis=dim)
    return value


def from_partner(value, axis, distance):
    mask = 2**distance
    pairs = [(source, source ^ mask) for source in range(lax.axis_size(axis))]
    return lax.ppermute(value, axis, pairs)


def laplace(field):
    return (
        field[..., 2:, 1:-1]
        + field[..., :-2, 1:-1]
        + field[..., 1:-1, 2:]
        + field[..., 1:-1, :-2]
        - 4.0 * field[..., 1:-1, 1:-1]
    )


def update_fields(extended, submerged_share, coriolis):
    temper = extended[0]
    saline = extended[1]
    eastward = extended[2]
    northward = extended[3]
    density = BETA * saline - ALPHA * temper
    pressure = GRAV_DZ * (jnp.cumsum(density, axis=0) - 0.5 * density)
    laplacian = laplace(extended)
    bilaplacian = laplace(laplacian)
    centre = extended[..., 2:-2, 2:-2]
    mixing = VISC_TWO * laplacian[..., 1:-1, 1:-1] - VISC_FOUR * bilaplacian
    grad_east = 0.5 * (pressure[:, 2:-2, 3:-1] - pressure[:, 2:-2, 1:-3])
    grad_north = 0.5 * (pressure[:, 3:-1, 2:-2] - pressure[:, 1:-3, 2:-2])
    tracers = extended[0:2]
    flux_east = tracers * eastward
    flux_north = tracers * northward
    advection = 0.5 * (flux_east[..., 2:-2, 3:-1] - flux_east[..., 2:-2, 1:-3]) + 0.5 * (
        flux_north[..., 3:-1, 2:-2] - flux_north[..., 1:-3, 2:-2]
    )
    accel_east = coriolis * centre[3] - grad_east
    accel_north = -coriolis * centre[2] - grad_north
    forcing = jnp.concatenate([-advection, accel_east[None], accel_north[None]], axis=0)
    return submerged_share * (centre + DT_STEP * (forcing + mixing))


RING_ROWS = 24
RING_COLS = 128


def _lap(a):
    rows, cols = a.shape
    return (
        pltpu.roll(a, rows - 1, 0)
        + pltpu.roll(a, 1, 0)
        + pltpu.roll(a, cols - 1, 1)
        + pltpu.roll(a, 1, 1)
        - 4.0 * a
    )


def _step_kernel(levels_ref, cor_ref, t_ref, s_ref, u_ref, v_ref, rows_ref, side_ref,
                 ot_ref, os_ref, ou_ref, ov_ref, ext_ref, cum_ref):
    k = pl.program_id(0)
    ny, nx = t_ref.shape[1], t_ref.shape[2]

    @pl.when(k == 0)
    def _():
        cum_ref[...] = jnp.zeros_like(cum_ref)

    wet = (levels_ref[...] > k).astype(jnp.float32)
    for c, ref in enumerate((t_ref, s_ref, u_ref, v_ref)):
        ext_ref[c, 0:ny, 0:nx] = ref[0] * wet
        ext_ref[c, ny:RING_ROWS, 0:nx] = rows_ref[0, c]
        ext_ref[c, :, nx:] = side_ref[0, c]

    def centre(a):
        return a[0:ny, 0:nx]

    def east(a):
        return centre(pltpu.roll(a, a.shape[1] - 1, 1))

    def west(a):
        return centre(pltpu.roll(a, 1, 1))

    def north(a):
        return centre(pltpu.roll(a, a.shape[0] - 1, 0))

    def south(a):
        return centre(pltpu.roll(a, 1, 0))

    temper = ext_ref[0]
    saline = ext_ref[1]
    density = BETA * saline - ALPHA * temper
    cum = cum_ref[...] + density
    cum_ref[...] = cum
    pressure = GRAV_DZ * (cum - 0.5 * density)
    grad_east = 0.5 * (east(pressure) - west(pressure))
    grad_north = 0.5 * (north(pressure) - south(pressure))
    eastward = ext_ref[2]
    northward = ext_ref[3]
    cor = cor_ref[...]
    outs = (ot_ref, os_ref, ou_ref, ov_ref)
    for c in range(4):
        field = ext_ref[c]
        lap = _lap(field)
        bil = (north(lap) + south(lap) + east(lap) + west(lap) - 4.0 * centre(lap))
        mixing = VISC_TWO * centre(lap) - VISC_FOUR * bil
        if c < 2:
            fe = field * eastward
            fn = field * northward
            adv = 0.5 * (east(fe) - west(fe)) + 0.5 * (north(fn) - south(fn))
            forcing = -adv
        elif c == 2:
            forcing = cor * centre(northward) - grad_east
        else:
            forcing = -cor * centre(eastward) - grad_north
        outs[c][0] = wet * (centre(field) + DT_STEP * (forcing + mixing))


def stencil_call(levels, cor, fields, rows, side):
    nz, ny, nx = fields[0].shape
    plane = pl.BlockSpec((1, ny, nx), lambda k: (k, 0, 0))
    fixed = pl.BlockSpec((ny, nx), lambda k: (0, 0))
    out_shape = [jax.ShapeDtypeStruct((nz, ny, nx), jnp.float32)] * 4
    return pl.pallas_call(
        _step_kernel,
        grid=(nz,),
        in_specs=[fixed, fixed, plane, plane, plane, plane,
                  pl.BlockSpec((1, 4, RING_ROWS - ny, nx), lambda k: (k, 0, 0, 0)),
                  pl.BlockSpec((1, 4, RING_ROWS, RING_COLS), lambda k: (k, 0, 0, 0))],
        out_specs=[plane] * 4,
        out_shape=out_shape,
        scratch_shapes=[pltpu.VMEM((4, RING_ROWS, nx + RING_COLS), jnp.float32),
                        pltpu.VMEM((RING_ROWS, nx + RING_COLS), jnp.float32)],
        compiler_params=pltpu.CompilerParams(dimension_semantics=("arbitrary",)),
    )(levels, cor, *fields, rows, side)


def pack_halo(from_south, north_rows, west, east):
    nc, nz, _, nx = from_south.shape
    gap = RING_ROWS - 16 - 4
    rows = jnp.concatenate(
        [north_rows, jnp.zeros((nc, nz, gap, nx), jnp.float32), from_south], axis=2)
    def circ(col):
        return jnp.concatenate(
            [col[:, :, 2:], jnp.zeros((nc, nz, RING_ROWS - col.shape[2], 2), jnp.float32), col[:, :, :2]],
            axis=2)
    side = jnp.concatenate(
        [circ(east), jnp.zeros((nc, nz, RING_ROWS, RING_COLS - 4), jnp.float32), circ(west)], axis=3)
    return jnp.swapaxes(rows, 0, 1), jnp.swapaxes(side, 0, 1)


def shift_pairs(count, step, wrap):
    pairs = []
    for i in range(count):
        j = i + step
        if wrap:
            pairs.append((i, j % count))
        elif 0 <= j < count:
            pairs.append((i, j))
    return pairs


def per_device(
    thermal_anomaly,
    saltiness_anomaly,
    zonal_velocity_array,
    meridional_velocity_array,
    seawater_profile_flags,
    submerged_layer_total,
    computed_block_flags,
):
    raw = (thermal_anomaly, saltiness_anomaly, zonal_velocity_array, meridional_velocity_array)
    block_depth_layers = thermal_anomaly.shape[0]
    block_meridional_extent = thermal_anomaly.shape[1]
    n_lon = lax.axis_size("lon")
    n_lat = lax.axis_size("lat")
    tile_alive = computed_block_flags[0, 0] == 1
    levels = jnp.where((seawater_profile_flags == 1) & tile_alive, submerged_layer_total, 0)
    depth_index = jnp.arange(block_depth_layers, dtype=jnp.int32)[:, None, None]

    def masked(rows, cols):
        wet = (depth_index < levels[None, rows, cols]).astype(jnp.float32)
        return jnp.stack([f[:, rows, cols] for f in raw]) * wet

    every = slice(None)
    top = masked(slice(-2, None), every)
    bottom = masked(slice(0, 2), every)
    from_south = lax.ppermute(top, "lat", shift_pairs(n_lat, 1, False))
    from_north = lax.ppermute(bottom, "lat", shift_pairs(n_lat, -1, False))
    last = n_lat - 1
    fold_pairs = [(p * n_lat + last, (n_lon - 1 - p) * n_lat + last) for p in range(n_lon)]
    folded = lax.ppermute(top, ("lon", "lat"), fold_pairs)
    signs = jnp.array([1.0, 1.0, -1.0, -1.0], jnp.float32).reshape(4, 1, 1, 1)
    fold_rows = folded[:, :, ::-1, ::-1] * signs
    is_northern = lax.axis_index("lat") == last
    north = jnp.where(is_northern, fold_rows, from_north)

    def tall(cols):
        return jnp.concatenate(
            [from_south[..., cols], masked(every, cols), north[..., cols]], axis=2)

    west = lax.ppermute(tall(slice(-2, None)), "lon", shift_pairs(n_lon, 1, True))
    east = lax.ppermute(tall(slice(0, 2)), "lon", shift_pairs(n_lon, -1, True))
    rows, side = pack_halo(from_south, north, west, east)
    total_rows = block_meridional_extent * n_lat
    row_pos = (
        lax.axis_index("lat") * block_meridional_extent
        + jnp.arange(block_meridional_extent, dtype=jnp.int32)
    ).astype(jnp.float32)
    coriolis = (CORIOLIS_MAX * jnp.sin(jnp.pi * ((row_pos + 0.5) / total_rows - 0.5)))[:, None]
    cor = jnp.broadcast_to(coriolis, levels.shape)
    return tuple(stencil_call(levels, cor, raw, rows, side))


def solution(mesh):
    return jax.shard_map(
        per_device,
        mesh=mesh,
        in_specs=(
            P(None, "lat", "lon"),
            P(None, "lat", "lon"),
            P(None, "lat", "lon"),
            P(None, "lat", "lon"),
            P("lat", "lon"),
            P("lat", "lon"),
            P("lat", "lon"),
        ),
        out_specs=(
            P(None, "lat", "lon"),
            P(None, "lat", "lon"),
            P(None, "lat", "lon"),
            P(None, "lat", "lon"),
        ),
        check_vma=False,
    )
```

```python
import jax
import jax.numpy as jnp
from jax import lax
from jax.sharding import PartitionSpec as P
from jax.experimental import pallas as pl
from jax.experimental.pallas import tpu as pltpu


ALPHA = 0.2
BETA = 0.8
GRAV_DZ = 0.1
DT_STEP = 0.2
VISC_TWO = 0.1
VISC_FOUR = 0.05
CORIOLIS_MAX = 0.3


def with_halo(value, sides, width, wrap):
    for axis, dim in sides:
        count, length = (lax.axis_size(axis), value.shape[dim])
        up = [(i, (i + 1) % count) for i in range(count if wrap else count - 1)]
        down = [(j, i) for i, j in up]
        last = lax.slice_in_dim(value, length - width, length, axis=dim)
        first = lax.slice_in_dim(value, 0, width, axis=dim)
        before = lax.ppermute(last, axis, up)
        after = lax.ppermute(first, axis, down)
        value = jnp.concatenate([before, value, after], axis=dim)
    return value


def from_partner(value, axis, distance):
    mask = 2**distance
    pairs = [(source, source ^ mask) for source in range(lax.axis_size(axis))]
    return lax.ppermute(value, axis, pairs)


def laplace(field):
    return (
        field[..., 2:, 1:-1]
        + field[..., :-2, 1:-1]
        + field[..., 1:-1, 2:]
        + field[..., 1:-1, :-2]
        - 4.0 * field[..., 1:-1, 1:-1]
    )


def update_fields(extended, submerged_share, coriolis):
    temper = extended[0]
    saline = extended[1]
    eastward = extended[2]
    northward = extended[3]
    density = BETA * saline - ALPHA * temper
    pressure = GRAV_DZ * (jnp.cumsum(density, axis=0) - 0.5 * density)
    laplacian = laplace(extended)
    bilaplacian = laplace(laplacian)
    centre = extended[..., 2:-2, 2:-2]
    mixing = VISC_TWO * laplacian[..., 1:-1, 1:-1] - VISC_FOUR * bilaplacian
    grad_east = 0.5 * (pressure[:, 2:-2, 3:-1] - pressure[:, 2:-2, 1:-3])
    grad_north = 0.5 * (pressure[:, 3:-1, 2:-2] - pressure[:, 1:-3, 2:-2])
    tracers = extended[0:2]
    flux_east = tracers * eastward
    flux_north = tracers * northward
    advection = 0.5 * (flux_east[..., 2:-2, 3:-1] - flux_east[..., 2:-2, 1:-3]) + 0.5 * (
        flux_north[..., 3:-1, 2:-2] - flux_north[..., 1:-3, 2:-2]
    )
    accel_east = coriolis * centre[3] - grad_east
    accel_north = -coriolis * centre[2] - grad_north
    forcing = jnp.concatenate([-advection, accel_east[None], accel_north[None]], axis=0)
    return submerged_share * (centre + DT_STEP * (forcing + mixing))


RING_ROWS = 24
RING_COLS = 128


def _lap(a):
    rows, cols = a.shape
    return (
        pltpu.roll(a, rows - 1, 0)
        + pltpu.roll(a, 1, 0)
        + pltpu.roll(a, cols - 1, 1)
        + pltpu.roll(a, 1, 1)
        - 4.0 * a
    )


def _step_kernel(levels_ref, cor_ref, t_ref, s_ref, u_ref, v_ref, north_ref, south_ref, side_ref,
                 ot_ref, os_ref, ou_ref, ov_ref, ext_ref, cum_ref):
    k = pl.program_id(0)
    ny, nx = t_ref.shape[1], t_ref.shape[2]

    @pl.when(k == 0)
    def _():
        cum_ref[...] = jnp.zeros_like(cum_ref)
        ext_ref[...] = jnp.zeros_like(ext_ref)

    wet = (levels_ref[...] > k).astype(jnp.float32)
    for c, ref in enumerate((t_ref, s_ref, u_ref, v_ref)):
        ext_ref[c, 0:ny, 0:nx] = ref[0] * wet
        ext_ref[c, ny:ny + 2, 0:nx] = north_ref[0, c]
        ext_ref[c, RING_ROWS - 2:RING_ROWS, 0:nx] = south_ref[0, c]
        ext_ref[c, :, nx:] = side_ref[0, c]

    def centre(a):
        return a[0:ny, 0:nx]

    def east(a):
        return centre(pltpu.roll(a, a.shape[1] - 1, 1))

    def west(a):
        return centre(pltpu.roll(a, 1, 1))

    def north(a):
        return centre(pltpu.roll(a, a.shape[0] - 1, 0))

    def south(a):
        return centre(pltpu.roll(a, 1, 0))

    temper = ext_ref[0]
    saline = ext_ref[1]
    density = BETA * saline - ALPHA * temper
    cum = cum_ref[...] + density
    cum_ref[...] = cum
    pressure = GRAV_DZ * (cum - 0.5 * density)
    grad_east = 0.5 * (east(pressure) - west(pressure))
    grad_north = 0.5 * (north(pressure) - south(pressure))
    eastward = ext_ref[2]
    northward = ext_ref[3]
    cor = cor_ref[...]
    outs = (ot_ref, os_ref, ou_ref, ov_ref)
    for c in range(4):
        field = ext_ref[c]
        lap = _lap(field)
        bil = (north(lap) + south(lap) + east(lap) + west(lap) - 4.0 * centre(lap))
        mixing = VISC_TWO * centre(lap) - VISC_FOUR * bil
        if c < 2:
            fe = field * eastward
            fn = field * northward
            adv = 0.5 * (east(fe) - west(fe)) + 0.5 * (north(fn) - south(fn))
            forcing = -adv
        elif c == 2:
            forcing = cor * centre(northward) - grad_east
        else:
            forcing = -cor * centre(eastward) - grad_north
        outs[c][0] = wet * (centre(field) + DT_STEP * (forcing + mixing))


def stencil_call(levels, cor, fields, north, south, side):
    nz, ny, nx = fields[0].shape
    plane = pl.BlockSpec((1, ny, nx), lambda k: (k, 0, 0))
    fixed = pl.BlockSpec((ny, nx), lambda k: (0, 0))
    rows = pl.BlockSpec((1, 4, 2, nx), lambda k: (k, 0, 0, 0))
    out_shape = [jax.ShapeDtypeStruct((nz, ny, nx), jnp.float32)] * 4
    return pl.pallas_call(
        _step_kernel,
        grid=(nz,),
        in_specs=[fixed, fixed, plane, plane, plane, plane, rows, rows,
                  pl.BlockSpec((1, 4, RING_ROWS, RING_COLS), lambda k: (k, 0, 0, 0))],
        out_specs=[plane] * 4,
        out_shape=out_shape,
        scratch_shapes=[pltpu.VMEM((4, RING_ROWS, nx + RING_COLS), jnp.float32),
                        pltpu.VMEM((RING_ROWS, nx + RING_COLS), jnp.float32)],
        compiler_params=pltpu.CompilerParams(dimension_semantics=("arbitrary",)),
    )(levels, cor, *fields, north, south, side)


def pack_side(west, east, sw, nw, se, ne):
    nc, nz, ny, _ = west.shape
    zero = jnp.zeros((nc, nz), jnp.float32)
    gap = jnp.zeros((nc, nz, RING_ROWS - ny - 2, 2), jnp.float32)

    def block(cols, top, bottom):
        return jnp.concatenate([cols, top[:, :, None, :], gap, bottom[:, :, None, :]], axis=2)

    east_block = block(east, jnp.stack([ne, zero], -1), jnp.stack([se, zero], -1))
    west_block = block(west, jnp.stack([zero, nw], -1), jnp.stack([zero, sw], -1))
    side = jnp.concatenate(
        [east_block, jnp.zeros((nc, nz, RING_ROWS, RING_COLS - 4), jnp.float32), west_block], axis=3)
    return jnp.swapaxes(side, 0, 1)


def flip_lanes(x):
    *lead, n = x.shape
    blocks = jnp.flip(x.reshape(*lead, n // 128, 128), axis=-2)
    lane = jnp.arange(128)
    anti = (lane[:, None] + lane[None, :] == 127).astype(jnp.float32)
    flipped = jnp.einsum("...i,ij->...j", blocks, anti, precision=lax.Precision.HIGHEST)
    return flipped.reshape(*lead, n)


def shift_pairs(count, step, wrap):
    pairs = []
    for i in range(count):
        j = i + step
        if wrap:
            pairs.append((i, j % count))
        elif 0 <= j < count:
            pairs.append((i, j))
    return pairs


def per_device(
    thermal_anomaly,
    saltiness_anomaly,
    zonal_velocity_array,
    meridional_velocity_array,
    seawater_profile_flags,
    submerged_layer_total,
    computed_block_flags,
):
    raw = (thermal_anomaly, saltiness_anomaly, zonal_velocity_array, meridional_velocity_array)
    block_depth_layers = thermal_anomaly.shape[0]
    block_meridional_extent = thermal_anomaly.shape[1]
    n_lon = lax.axis_size("lon")
    n_lat = lax.axis_size("lat")
    tile_alive = computed_block_flags[0, 0] == 1
    levels = jnp.where((seawater_profile_flags == 1) & tile_alive, submerged_layer_total, 0)
    depth_index = jnp.arange(block_depth_layers, dtype=jnp.int32)[:, None, None]

    def masked(rows, cols):
        wet = (depth_index < levels[None, rows, cols]).astype(jnp.float32)
        return jnp.stack([f[:, rows, cols] for f in raw]) * wet

    every = slice(None)
    last = n_lat - 1
    both = ("lon", "lat")

    def at(lon, lat):
        return (lon % n_lon) * n_lat + lat

    top = masked(slice(-2, None), every)
    fold_pairs = [(at(p, last), at(n_lon - 1 - p, last)) for p in range(n_lon)]
    folded = lax.ppermute(top, both, fold_pairs)
    bottom = masked(slice(0, 2), every)
    from_south = lax.ppermute(top, "lat", shift_pairs(n_lat, 1, False))
    from_north = lax.ppermute(bottom, "lat", shift_pairs(n_lat, -1, False))
    west = lax.ppermute(masked(every, slice(-2, None)), "lon", shift_pairs(n_lon, 1, True))
    east = lax.ppermute(masked(every, slice(0, 2)), "lon", shift_pairs(n_lon, -1, True))
    def cell(row, col):
        return masked(slice(row, row + 1), slice(col, col + 1))[:, :, 0, 0]

    ny, nx = block_meridional_extent, thermal_anomaly.shape[2]
    top_left = cell(ny - 1, 0)
    top_right = cell(ny - 1, nx - 1)
    bottom_left = cell(0, 0)
    bottom_right = cell(0, nx - 1)
    lats = range(n_lat)
    lons = range(n_lon)
    sw = lax.ppermute(top_right, both, [(at(t, l), at(t + 1, l + 1)) for t in lons for l in lats if l < last])
    se = lax.ppermute(top_left, both, [(at(t, l), at(t - 1, l + 1)) for t in lons for l in lats if l < last])
    nw = lax.ppermute(bottom_right, both, [(at(t, l), at(t + 1, l - 1)) for t in lons for l in lats if l > 0])
    ne = lax.ppermute(bottom_left, both, [(at(t, l), at(t - 1, l - 1)) for t in lons for l in lats if l > 0])
    fold_nw = lax.ppermute(top_left, both, [(at(p, last), at(n_lon - p, last)) for p in lons])
    fold_ne = lax.ppermute(top_right, both, [(at(p, last), at(n_lon - 2 - p, last)) for p in lons])
    signs = jnp.array([1.0, 1.0, -1.0, -1.0], jnp.float32)
    is_northern = lax.axis_index("lat") == last
    nw = jnp.where(is_northern, fold_nw * signs[:, None], nw)
    ne = jnp.where(is_northern, fold_ne * signs[:, None], ne)
    side = pack_side(west, east, sw, nw, se, ne)
    fold_rows = flip_lanes(folded[:, :, ::-1, :]) * signs[:, None, None, None]
    north = jnp.where(is_northern, fold_rows, from_north)
    total_rows = block_meridional_extent * n_lat
    row_pos = (
        lax.axis_index("lat") * block_meridional_extent
        + jnp.arange(block_meridional_extent, dtype=jnp.int32)
    ).astype(jnp.float32)
    coriolis = (CORIOLIS_MAX * jnp.sin(jnp.pi * ((row_pos + 0.5) / total_rows - 0.5)))[:, None]
    cor = jnp.broadcast_to(coriolis, levels.shape)
    return tuple(stencil_call(levels, cor, raw, jnp.swapaxes(north, 0, 1),
                              jnp.swapaxes(from_south, 0, 1), side))


def solution(mesh):
    return jax.shard_map(
        per_device,
        mesh=mesh,
        in_specs=(
            P(None, "lat", "lon"),
            P(None, "lat", "lon"),
            P(None, "lat", "lon"),
            P(None, "lat", "lon"),
            P("lat", "lon"),
            P("lat", "lon"),
            P("lat", "lon"),
        ),
        out_specs=(
            P(None, "lat", "lon"),
            P(None, "lat", "lon"),
            P(None, "lat", "lon"),
            P(None, "lat", "lon"),
        ),
        check_vma=False,
    )
```

```python
import jax
import jax.numpy as jnp
from jax import lax
from jax.sharding import PartitionSpec as P
from jax.experimental import pallas as pl
from jax.experimental.pallas import tpu as pltpu


ALPHA = 0.2
BETA = 0.8
GRAV_DZ = 0.1
DT_STEP = 0.2
VISC_TWO = 0.1
VISC_FOUR = 0.05
CORIOLIS_MAX = 0.3


def with_halo(value, sides, width, wrap):
    for axis, dim in sides:
        count, length = (lax.axis_size(axis), value.shape[dim])
        up = [(i, (i + 1) % count) for i in range(count if wrap else count - 1)]
        down = [(j, i) for i, j in up]
        last = lax.slice_in_dim(value, length - width, length, axis=dim)
        first = lax.slice_in_dim(value, 0, width, axis=dim)
        before = lax.ppermute(last, axis, up)
        after = lax.ppermute(first, axis, down)
        value = jnp.concatenate([before, value, after], axis=dim)
    return value


def from_partner(value, axis, distance):
    mask = 2**distance
    pairs = [(source, source ^ mask) for source in range(lax.axis_size(axis))]
    return lax.ppermute(value, axis, pairs)


def laplace(field):
    return (
        field[..., 2:, 1:-1]
        + field[..., :-2, 1:-1]
        + field[..., 1:-1, 2:]
        + field[..., 1:-1, :-2]
        - 4.0 * field[..., 1:-1, 1:-1]
    )


def update_fields(extended, submerged_share, coriolis):
    temper = extended[0]
    saline = extended[1]
    eastward = extended[2]
    northward = extended[3]
    density = BETA * saline - ALPHA * temper
    pressure = GRAV_DZ * (jnp.cumsum(density, axis=0) - 0.5 * density)
    laplacian = laplace(extended)
    bilaplacian = laplace(laplacian)
    centre = extended[..., 2:-2, 2:-2]
    mixing = VISC_TWO * laplacian[..., 1:-1, 1:-1] - VISC_FOUR * bilaplacian
    grad_east = 0.5 * (pressure[:, 2:-2, 3:-1] - pressure[:, 2:-2, 1:-3])
    grad_north = 0.5 * (pressure[:, 3:-1, 2:-2] - pressure[:, 1:-3, 2:-2])
    tracers = extended[0:2]
    flux_east = tracers * eastward
    flux_north = tracers * northward
    advection = 0.5 * (flux_east[..., 2:-2, 3:-1] - flux_east[..., 2:-2, 1:-3]) + 0.5 * (
        flux_north[..., 3:-1, 2:-2] - flux_north[..., 1:-3, 2:-2]
    )
    accel_east = coriolis * centre[3] - grad_east
    accel_north = -coriolis * centre[2] - grad_north
    forcing = jnp.concatenate([-advection, accel_east[None], accel_north[None]], axis=0)
    return submerged_share * (centre + DT_STEP * (forcing + mixing))


RING_ROWS = 24
RING_COLS = 128


def _lap(a):
    rows, cols = a.shape
    return (
        pltpu.roll(a, rows - 1, 0)
        + pltpu.roll(a, 1, 0)
        + pltpu.roll(a, cols - 1, 1)
        + pltpu.roll(a, 1, 1)
        - 4.0 * a
    )


def _step_kernel(levels_ref, cor_ref, t_ref, s_ref, u_ref, v_ref, north_ref, south_ref, side_ref,
                 ot_ref, os_ref, ou_ref, ov_ref, ext_ref, cum_ref):
    k = pl.program_id(0)
    ny, nx = t_ref.shape[1], t_ref.shape[2]

    @pl.when(k == 0)
    def _():
        cum_ref[...] = jnp.zeros_like(cum_ref)
        ext_ref[...] = jnp.zeros_like(ext_ref)

    wet = (levels_ref[...] > k).astype(jnp.float32)
    for c, ref in enumerate((t_ref, s_ref, u_ref, v_ref)):
        ext_ref[c, 0:ny, 0:nx] = ref[0] * wet
        ext_ref[c, ny:ny + 2, 0:nx] = north_ref[0, c]
        ext_ref[c, RING_ROWS - 2:RING_ROWS, 0:nx] = south_ref[0, c]
        ext_ref[c, :, nx:] = side_ref[0, c]

    def centre(a):
        return a[0:ny, 0:nx]

    def east(a):
        return centre(pltpu.roll(a, a.shape[1] - 1, 1))

    def west(a):
        return centre(pltpu.roll(a, 1, 1))

    def north(a):
        return centre(pltpu.roll(a, a.shape[0] - 1, 0))

    def south(a):
        return centre(pltpu.roll(a, 1, 0))

    temper = ext_ref[0]
    saline = ext_ref[1]
    density = BETA * saline - ALPHA * temper
    cum = cum_ref[...] + density
    cum_ref[...] = cum
    pressure = GRAV_DZ * (cum - 0.5 * density)
    grad_east = 0.5 * (east(pressure) - west(pressure))
    grad_north = 0.5 * (north(pressure) - south(pressure))
    eastward = ext_ref[2]
    northward = ext_ref[3]
    cor = cor_ref[...]
    outs = (ot_ref, os_ref, ou_ref, ov_ref)
    for c in range(4):
        field = ext_ref[c]
        lap = _lap(field)
        bil = (north(lap) + south(lap) + east(lap) + west(lap) - 4.0 * centre(lap))
        mixing = VISC_TWO * centre(lap) - VISC_FOUR * bil
        if c < 2:
            fe = field * eastward
            fn = field * northward
            adv = 0.5 * (east(fe) - west(fe)) + 0.5 * (north(fn) - south(fn))
            forcing = -adv
        elif c == 2:
            forcing = cor * centre(northward) - grad_east
        else:
            forcing = -cor * centre(eastward) - grad_north
        outs[c][0] = wet * (centre(field) + DT_STEP * (forcing + mixing))


def stencil_call(levels, cor, fields, north, south, side):
    nz, ny, nx = fields[0].shape
    plane = pl.BlockSpec((1, ny, nx), lambda k: (k, 0, 0))
    fixed = pl.BlockSpec((ny, nx), lambda k: (0, 0))
    rows = pl.BlockSpec((1, 4, 2, nx), lambda k: (k, 0, 0, 0))
    out_shape = [jax.ShapeDtypeStruct((nz, ny, nx), jnp.float32)] * 4
    return pl.pallas_call(
        _step_kernel,
        grid=(nz,),
        in_specs=[fixed, fixed, plane, plane, plane, plane, rows, rows,
                  pl.BlockSpec((1, 4, RING_ROWS, RING_COLS), lambda k: (k, 0, 0, 0))],
        out_specs=[plane] * 4,
        out_shape=out_shape,
        scratch_shapes=[pltpu.VMEM((4, RING_ROWS, nx + RING_COLS), jnp.float32),
                        pltpu.VMEM((RING_ROWS, nx + RING_COLS), jnp.float32)],
        compiler_params=pltpu.CompilerParams(dimension_semantics=("arbitrary",)),
    )(levels, cor, *fields, north, south, side)


def pack_side(west, east, sw, nw, se, ne):
    nc, nz, ny, _ = west.shape
    zero = jnp.zeros((nc, nz), jnp.float32)
    gap = jnp.zeros((nc, nz, RING_ROWS - ny - 2, 2), jnp.float32)

    def block(cols, top, bottom):
        return jnp.concatenate([cols, top[:, :, None, :], gap, bottom[:, :, None, :]], axis=2)

    east_block = block(east, jnp.stack([ne, zero], -1), jnp.stack([se, zero], -1))
    west_block = block(west, jnp.stack([zero, nw], -1), jnp.stack([zero, sw], -1))
    side = jnp.concatenate(
        [east_block, jnp.zeros((nc, nz, RING_ROWS, RING_COLS - 4), jnp.float32), west_block], axis=3)
    return jnp.swapaxes(side, 0, 1)


def flip_rows_lanes(x):
    *lead, rows, n = x.shape
    lane = jnp.arange(128)
    anti = (lane[:, None] + lane[None, :] == 127).astype(jnp.float32)
    flipped = jnp.einsum("...i,ij->...j", x.reshape(*lead, rows, n // 128, 128), anti,
                         precision=lax.Precision.HIGHEST)
    pieces = [flipped[..., r:r + 1, b, :] for r in reversed(range(rows)) for b in reversed(range(n // 128))]
    return jnp.concatenate(pieces, axis=-1).reshape(*lead, rows, n)


def shift_pairs(count, step, wrap):
    pairs = []
    for i in range(count):
        j = i + step
        if wrap:
            pairs.append((i, j % count))
        elif 0 <= j < count:
            pairs.append((i, j))
    return pairs


def per_device(
    thermal_anomaly,
    saltiness_anomaly,
    zonal_velocity_array,
    meridional_velocity_array,
    seawater_profile_flags,
    submerged_layer_total,
    computed_block_flags,
):
    raw = (thermal_anomaly, saltiness_anomaly, zonal_velocity_array, meridional_velocity_array)
    block_depth_layers = thermal_anomaly.shape[0]
    block_meridional_extent = thermal_anomaly.shape[1]
    n_lon = lax.axis_size("lon")
    n_lat = lax.axis_size("lat")
    tile_alive = computed_block_flags[0, 0] == 1
    levels = jnp.where((seawater_profile_flags == 1) & tile_alive, submerged_layer_total, 0)
    depth_index = jnp.arange(block_depth_layers, dtype=jnp.int32)[:, None, None]

    def masked(rows, cols):
        wet = (depth_index < levels[None, rows, cols]).astype(jnp.float32)
        return jnp.stack([f[:, rows, cols] for f in raw]) * wet

    every = slice(None)
    last = n_lat - 1
    top = masked(slice(-2, None), every)
    fold_pairs = [(p * n_lat + last, (n_lon - 1 - p) * n_lat + last) for p in range(n_lon)]
    folded = lax.ppermute(top, ("lon", "lat"), fold_pairs)
    bottom = masked(slice(0, 2), every)
    from_south = lax.ppermute(top, "lat", shift_pairs(n_lat, 1, False))
    from_north = lax.ppermute(bottom, "lat", shift_pairs(n_lat, -1, False))
    signs = jnp.array([1.0, 1.0, -1.0, -1.0], jnp.float32).reshape(4, 1, 1, 1)
    fold_rows = flip_rows_lanes(folded) * signs
    is_northern = lax.axis_index("lat") == last
    north = jnp.where(is_northern, fold_rows, from_north)

    def tall(cols):
        return jnp.concatenate(
            [from_south[..., cols], masked(every, cols), north[..., cols]], axis=2)

    west = lax.ppermute(tall(slice(-2, None)), "lon", shift_pairs(n_lon, 1, True))
    east = lax.ppermute(tall(slice(0, 2)), "lon", shift_pairs(n_lon, -1, True))
    side = pack_side(west[:, :, 2:-2], east[:, :, 2:-2], west[:, :, 1, 1], west[:, :, -2, 1],
                     east[:, :, 1, 0], east[:, :, -2, 0])
    total_rows = block_meridional_extent * n_lat
    row_pos = (
        lax.axis_index("lat") * block_meridional_extent
        + jnp.arange(block_meridional_extent, dtype=jnp.int32)
    ).astype(jnp.float32)
    coriolis = (CORIOLIS_MAX * jnp.sin(jnp.pi * ((row_pos + 0.5) / total_rows - 0.5)))[:, None]
    cor = jnp.broadcast_to(coriolis, levels.shape)
    return tuple(stencil_call(levels, cor, raw, jnp.swapaxes(north, 0, 1),
                              jnp.swapaxes(from_south, 0, 1), side))


def solution(mesh):
    return jax.shard_map(
        per_device,
        mesh=mesh,
        in_specs=(
            P(None, "lat", "lon"),
            P(None, "lat", "lon"),
            P(None, "lat", "lon"),
            P(None, "lat", "lon"),
            P("lat", "lon"),
            P("lat", "lon"),
            P("lat", "lon"),
        ),
        out_specs=(
            P(None, "lat", "lon"),
            P(None, "lat", "lon"),
            P(None, "lat", "lon"),
            P(None, "lat", "lon"),
        ),
        check_vma=False,
    )
```

```python
import jax
import jax.numpy as jnp
from jax import lax
from jax.sharding import PartitionSpec as P
from jax.experimental import pallas as pl
from jax.experimental.pallas import tpu as pltpu


ALPHA = 0.2
BETA = 0.8
GRAV_DZ = 0.1
DT_STEP = 0.2
VISC_TWO = 0.1
VISC_FOUR = 0.05
CORIOLIS_MAX = 0.3


def with_halo(value, sides, width, wrap):
    for axis, dim in sides:
        count, length = (lax.axis_size(axis), value.shape[dim])
        up = [(i, (i + 1) % count) for i in range(count if wrap else count - 1)]
        down = [(j, i) for i, j in up]
        last = lax.slice_in_dim(value, length - width, length, axis=dim)
        first = lax.slice_in_dim(value, 0, width, axis=dim)
        before = lax.ppermute(last, axis, up)
        after = lax.ppermute(first, axis, down)
        value = jnp.concatenate([before, value, after], axis=dim)
    return value


def from_partner(value, axis, distance):
    mask = 2**distance
    pairs = [(source, source ^ mask) for source in range(lax.axis_size(axis))]
    return lax.ppermute(value, axis, pairs)


def laplace(field):
    return (
        field[..., 2:, 1:-1]
        + field[..., :-2, 1:-1]
        + field[..., 1:-1, 2:]
        + field[..., 1:-1, :-2]
        - 4.0 * field[..., 1:-1, 1:-1]
    )


def update_fields(extended, submerged_share, coriolis):
    temper = extended[0]
    saline = extended[1]
    eastward = extended[2]
    northward = extended[3]
    density = BETA * saline - ALPHA * temper
    pressure = GRAV_DZ * (jnp.cumsum(density, axis=0) - 0.5 * density)
    laplacian = laplace(extended)
    bilaplacian = laplace(laplacian)
    centre = extended[..., 2:-2, 2:-2]
    mixing = VISC_TWO * laplacian[..., 1:-1, 1:-1] - VISC_FOUR * bilaplacian
    grad_east = 0.5 * (pressure[:, 2:-2, 3:-1] - pressure[:, 2:-2, 1:-3])
    grad_north = 0.5 * (pressure[:, 3:-1, 2:-2] - pressure[:, 1:-3, 2:-2])
    tracers = extended[0:2]
    flux_east = tracers * eastward
    flux_north = tracers * northward
    advection = 0.5 * (flux_east[..., 2:-2, 3:-1] - flux_east[..., 2:-2, 1:-3]) + 0.5 * (
        flux_north[..., 3:-1, 2:-2] - flux_north[..., 1:-3, 2:-2]
    )
    accel_east = coriolis * centre[3] - grad_east
    accel_north = -coriolis * centre[2] - grad_north
    forcing = jnp.concatenate([-advection, accel_east[None], accel_north[None]], axis=0)
    return submerged_share * (centre + DT_STEP * (forcing + mixing))


RING_ROWS = 24
RING_COLS = 128


def _lap(a):
    rows, cols = a.shape
    return (
        pltpu.roll(a, rows - 1, 0)
        + pltpu.roll(a, 1, 0)
        + pltpu.roll(a, cols - 1, 1)
        + pltpu.roll(a, 1, 1)
        - 4.0 * a
    )


def _step_kernel(levels_ref, cor_ref, t_ref, s_ref, u_ref, v_ref, north_ref, fold_ref, south_ref, side_ref,
                 ot_ref, os_ref, ou_ref, ov_ref, ext_ref, cum_ref):
    k = pl.program_id(0)
    ny, nx = t_ref.shape[1], t_ref.shape[2]

    @pl.when(k == 0)
    def _():
        cum_ref[...] = jnp.zeros_like(cum_ref)
        ext_ref[...] = jnp.zeros_like(ext_ref)

    wet = (levels_ref[...] > k).astype(jnp.float32)
    for c, ref in enumerate((t_ref, s_ref, u_ref, v_ref)):
        ext_ref[c, 0:ny, 0:nx] = ref[0] * wet
        for r in range(2):
            for b in range(nx // RING_COLS):
                src_cols = slice(nx - (b + 1) * RING_COLS, nx - b * RING_COLS)
                dst_cols = slice(b * RING_COLS, (b + 1) * RING_COLS)
                ext_ref[c, ny + r:ny + r + 1, dst_cols] = (
                    north_ref[0, c, r:r + 1, dst_cols] + fold_ref[0, c, 1 - r:2 - r, src_cols])
        ext_ref[c, RING_ROWS - 2:RING_ROWS, 0:nx] = south_ref[0, c]
        ext_ref[c, :, nx:] = side_ref[0, c]

    def centre(a):
        return a[0:ny, 0:nx]

    def east(a):
        return centre(pltpu.roll(a, a.shape[1] - 1, 1))

    def west(a):
        return centre(pltpu.roll(a, 1, 1))

    def north(a):
        return centre(pltpu.roll(a, a.shape[0] - 1, 0))

    def south(a):
        return centre(pltpu.roll(a, 1, 0))

    temper = ext_ref[0]
    saline = ext_ref[1]
    density = BETA * saline - ALPHA * temper
    cum = cum_ref[...] + density
    cum_ref[...] = cum
    pressure = GRAV_DZ * (cum - 0.5 * density)
    grad_east = 0.5 * (east(pressure) - west(pressure))
    grad_north = 0.5 * (north(pressure) - south(pressure))
    eastward = ext_ref[2]
    northward = ext_ref[3]
    cor = cor_ref[...]
    outs = (ot_ref, os_ref, ou_ref, ov_ref)
    for c in range(4):
        field = ext_ref[c]
        lap = _lap(field)
        bil = (north(lap) + south(lap) + east(lap) + west(lap) - 4.0 * centre(lap))
        mixing = VISC_TWO * centre(lap) - VISC_FOUR * bil
        if c < 2:
            fe = field * eastward
            fn = field * northward
            adv = 0.5 * (east(fe) - west(fe)) + 0.5 * (north(fn) - south(fn))
            forcing = -adv
        elif c == 2:
            forcing = cor * centre(northward) - grad_east
        else:
            forcing = -cor * centre(eastward) - grad_north
        outs[c][0] = wet * (centre(field) + DT_STEP * (forcing + mixing))


def stencil_call(levels, cor, fields, north, fold, south, side):
    nz, ny, nx = fields[0].shape
    plane = pl.BlockSpec((1, ny, nx), lambda k: (k, 0, 0))
    fixed = pl.BlockSpec((ny, nx), lambda k: (0, 0))
    rows = pl.BlockSpec((1, 4, 2, nx), lambda k: (k, 0, 0, 0))
    out_shape = [jax.ShapeDtypeStruct((nz, ny, nx), jnp.float32)] * 4
    return pl.pallas_call(
        _step_kernel,
        grid=(nz,),
        in_specs=[fixed, fixed, plane, plane, plane, plane, rows, rows, rows,
                  pl.BlockSpec((1, 4, RING_ROWS, RING_COLS), lambda k: (k, 0, 0, 0))],
        out_specs=[plane] * 4,
        out_shape=out_shape,
        scratch_shapes=[pltpu.VMEM((4, RING_ROWS, nx + RING_COLS), jnp.float32),
                        pltpu.VMEM((RING_ROWS, nx + RING_COLS), jnp.float32)],
        compiler_params=pltpu.CompilerParams(dimension_semantics=("arbitrary",)),
    )(levels, cor, *fields, north, fold, south, side)


def pack_side(west, east, sw, nw, se, ne):
    nc, nz, ny, _ = west.shape
    zero = jnp.zeros((nc, nz), jnp.float32)
    gap = jnp.zeros((nc, nz, RING_ROWS - ny - 2, 2), jnp.float32)

    def block(cols, top, bottom):
        return jnp.concatenate([cols, top[:, :, None, :], gap, bottom[:, :, None, :]], axis=2)

    east_block = block(east, jnp.stack([ne, zero], -1), jnp.stack([se, zero], -1))
    west_block = block(west, jnp.stack([zero, nw], -1), jnp.stack([zero, sw], -1))
    side = jnp.concatenate(
        [east_block, jnp.zeros((nc, nz, RING_ROWS, RING_COLS - 4), jnp.float32), west_block], axis=3)
    return jnp.swapaxes(side, 0, 1)


def flip_lanes_in_blocks(x):
    *lead, n = x.shape
    lane = jnp.arange(128)
    anti = lax.optimization_barrier((lane[:, None] + lane[None, :] == 127).astype(jnp.float32))
    flipped = jnp.einsum("...i,ij->...j", x.reshape(*lead, n // 128, 128), anti,
                         precision=lax.Precision.HIGHEST)
    return flipped.reshape(*lead, n)


def shift_pairs(count, step, wrap):
    pairs = []
    for i in range(count):
        j = i + step
        if wrap:
            pairs.append((i, j % count))
        elif 0 <= j < count:
            pairs.append((i, j))
    return pairs


def per_device(
    thermal_anomaly,
    saltiness_anomaly,
    zonal_velocity_array,
    meridional_velocity_array,
    seawater_profile_flags,
    submerged_layer_total,
    computed_block_flags,
):
    raw = (thermal_anomaly, saltiness_anomaly, zonal_velocity_array, meridional_velocity_array)
    block_depth_layers = thermal_anomaly.shape[0]
    block_meridional_extent = thermal_anomaly.shape[1]
    n_lon = lax.axis_size("lon")
    n_lat = lax.axis_size("lat")
    tile_alive = computed_block_flags[0, 0] == 1
    levels = jnp.where((seawater_profile_flags == 1) & tile_alive, submerged_layer_total, 0)
    depth_index = jnp.arange(block_depth_layers, dtype=jnp.int32)[:, None, None]

    def masked(rows, cols):
        wet = (depth_index < levels[None, rows, cols]).astype(jnp.float32)
        return jnp.stack([f[:, rows, cols] for f in raw]) * wet

    every = slice(None)
    last = n_lat - 1
    both = ("lon", "lat")
    ny, nx = block_meridional_extent, thermal_anomaly.shape[2]

    def at(lon, lat):
        return (lon % n_lon) * n_lat + lat

    def cell(row, col):
        return masked(slice(row, row + 1), slice(col, col + 1))[:, :, 0, 0]

    top = masked(slice(-2, None), every)
    folded = lax.ppermute(top, both, [(at(p, last), at(n_lon - 1 - p, last)) for p in range(n_lon)])
    fold_nw = lax.ppermute(cell(ny - 1, 0), both, [(at(p, last), at(n_lon - p, last)) for p in range(n_lon)])
    fold_ne = lax.ppermute(cell(ny - 1, nx - 1), both,
                           [(at(p, last), at(n_lon - 2 - p, last)) for p in range(n_lon)])
    bottom = masked(slice(0, 2), every)
    from_south = lax.ppermute(top, "lat", shift_pairs(n_lat, 1, False))
    from_north = lax.ppermute(bottom, "lat", shift_pairs(n_lat, -1, False))

    def tall(cols):
        return jnp.concatenate(
            [from_south[..., cols], masked(every, cols), from_north[..., cols]], axis=2)

    west = lax.ppermute(tall(slice(-2, None)), "lon", shift_pairs(n_lon, 1, True))
    east = lax.ppermute(tall(slice(0, 2)), "lon", shift_pairs(n_lon, -1, True))
    signs = jnp.array([1.0, 1.0, -1.0, -1.0], jnp.float32)
    is_northern = lax.axis_index("lat") == last
    nw = jnp.where(is_northern, fold_nw * signs[:, None], west[:, :, -2, 1])
    ne = jnp.where(is_northern, fold_ne * signs[:, None], east[:, :, -2, 0])
    side = pack_side(west[:, :, 2:-2], east[:, :, 2:-2], west[:, :, 1, 1], nw, east[:, :, 1, 0], ne)
    fold_rows = flip_lanes_in_blocks(folded) * signs[:, None, None, None]
    total_rows = block_meridional_extent * n_lat
    row_pos = (
        lax.axis_index("lat") * block_meridional_extent
        + jnp.arange(block_meridional_extent, dtype=jnp.int32)
    ).astype(jnp.float32)
    coriolis = (CORIOLIS_MAX * jnp.sin(jnp.pi * ((row_pos + 0.5) / total_rows - 0.5)))[:, None]
    cor = jnp.broadcast_to(coriolis, levels.shape)
    return tuple(stencil_call(levels, cor, raw, jnp.swapaxes(from_north, 0, 1), jnp.swapaxes(fold_rows, 0, 1),
                              jnp.swapaxes(from_south, 0, 1), side))


def solution(mesh):
    return jax.shard_map(
        per_device,
        mesh=mesh,
        in_specs=(
            P(None, "lat", "lon"),
            P(None, "lat", "lon"),
            P(None, "lat", "lon"),
            P(None, "lat", "lon"),
            P("lat", "lon"),
            P("lat", "lon"),
            P("lat", "lon"),
        ),
        out_specs=(
            P(None, "lat", "lon"),
            P(None, "lat", "lon"),
            P(None, "lat", "lon"),
            P(None, "lat", "lon"),
        ),
        check_vma=False,
    )
```

```python
import jax
import jax.numpy as jnp
from jax import lax
from jax.sharding import PartitionSpec as P
from jax.experimental import pallas as pl
from jax.experimental.pallas import tpu as pltpu


ALPHA = 0.2
BETA = 0.8
GRAV_DZ = 0.1
DT_STEP = 0.2
VISC_TWO = 0.1
VISC_FOUR = 0.05
CORIOLIS_MAX = 0.3


def with_halo(value, sides, width, wrap):
    for axis, dim in sides:
        count, length = (lax.axis_size(axis), value.shape[dim])
        up = [(i, (i + 1) % count) for i in range(count if wrap else count - 1)]
        down = [(j, i) for i, j in up]
        last = lax.slice_in_dim(value, length - width, length, axis=dim)
        first = lax.slice_in_dim(value, 0, width, axis=dim)
        before = lax.ppermute(last, axis, up)
        after = lax.ppermute(first, axis, down)
        value = jnp.concatenate([before, value, after], axis=dim)
    return value


def from_partner(value, axis, distance):
    mask = 2**distance
    pairs = [(source, source ^ mask) for source in range(lax.axis_size(axis))]
    return lax.ppermute(value, axis, pairs)


def laplace(field):
    return (
        field[..., 2:, 1:-1]
        + field[..., :-2, 1:-1]
        + field[..., 1:-1, 2:]
        + field[..., 1:-1, :-2]
        - 4.0 * field[..., 1:-1, 1:-1]
    )


def update_fields(extended, submerged_share, coriolis):
    temper = extended[0]
    saline = extended[1]
    eastward = extended[2]
    northward = extended[3]
    density = BETA * saline - ALPHA * temper
    pressure = GRAV_DZ * (jnp.cumsum(density, axis=0) - 0.5 * density)
    laplacian = laplace(extended)
    bilaplacian = laplace(laplacian)
    centre = extended[..., 2:-2, 2:-2]
    mixing = VISC_TWO * laplacian[..., 1:-1, 1:-1] - VISC_FOUR * bilaplacian
    grad_east = 0.5 * (pressure[:, 2:-2, 3:-1] - pressure[:, 2:-2, 1:-3])
    grad_north = 0.5 * (pressure[:, 3:-1, 2:-2] - pressure[:, 1:-3, 2:-2])
    tracers = extended[0:2]
    flux_east = tracers * eastward
    flux_north = tracers * northward
    advection = 0.5 * (flux_east[..., 2:-2, 3:-1] - flux_east[..., 2:-2, 1:-3]) + 0.5 * (
        flux_north[..., 3:-1, 2:-2] - flux_north[..., 1:-3, 2:-2]
    )
    accel_east = coriolis * centre[3] - grad_east
    accel_north = -coriolis * centre[2] - grad_north
    forcing = jnp.concatenate([-advection, accel_east[None], accel_north[None]], axis=0)
    return submerged_share * (centre + DT_STEP * (forcing + mixing))


RING_ROWS = 24
RING_COLS = 128


def _lap(a):
    rows, cols = a.shape
    return (
        pltpu.roll(a, rows - 1, 0)
        + pltpu.roll(a, 1, 0)
        + pltpu.roll(a, cols - 1, 1)
        + pltpu.roll(a, 1, 1)
        - 4.0 * a
    )


def _physics(ext_ref, cum_ref, which, cor, wet, rows):
    nx = ext_ref.shape[2] - RING_COLS

    def centre(a):
        return a[0:rows, 0:nx]

    def east(a):
        return centre(pltpu.roll(a, a.shape[1] - 1, 1))

    def west(a):
        return centre(pltpu.roll(a, 1, 1))

    def north(a):
        return centre(pltpu.roll(a, a.shape[0] - 1, 0))

    def south(a):
        return centre(pltpu.roll(a, 1, 0))

    temper = ext_ref[0]
    saline = ext_ref[1]
    density = BETA * saline - ALPHA * temper
    cum = cum_ref[which] + density
    cum_ref[which] = cum
    pressure = GRAV_DZ * (cum - 0.5 * density)
    grad_east = 0.5 * (east(pressure) - west(pressure))
    grad_north = 0.5 * (north(pressure) - south(pressure))
    eastward = ext_ref[2]
    northward = ext_ref[3]
    results = []
    for c in range(4):
        field = ext_ref[c]
        lap = _lap(field)
        bil = (north(lap) + south(lap) + east(lap) + west(lap) - 4.0 * centre(lap))
        mixing = VISC_TWO * centre(lap) - VISC_FOUR * bil
        if c < 2:
            fe = field * eastward
            fn = field * northward
            adv = 0.5 * (east(fe) - west(fe)) + 0.5 * (north(fn) - south(fn))
            forcing = -adv
        elif c == 2:
            forcing = cor * centre(northward) - grad_east
        else:
            forcing = -cor * centre(eastward) - grad_north
        results.append(wet * (centre(field) + DT_STEP * (forcing + mixing)))
    return results


def _interior_kernel(levels_ref, cor_ref, t_ref, s_ref, u_ref, v_ref, side_ref,
                     ot_ref, os_ref, ou_ref, ov_ref, ext_ref, cum_ref):
    k = pl.program_id(0)
    ny, nx = t_ref.shape[1], t_ref.shape[2]

    @pl.when(k == 0)
    def _():
        cum_ref[...] = jnp.zeros_like(cum_ref)
        ext_ref[...] = jnp.zeros_like(ext_ref)

    wet = (levels_ref[...] > k).astype(jnp.float32)
    for c, ref in enumerate((t_ref, s_ref, u_ref, v_ref)):
        ext_ref[c, 0:ny, 0:nx] = ref[0] * wet
        ext_ref[c, :, nx:] = side_ref[0, c]
    results = _physics(ext_ref, cum_ref, 0, cor_ref[...], wet, ny)
    for o, res in zip((ot_ref, os_ref, ou_ref, ov_ref), results):
        o[0] = res


def interior_call(levels, cor, fields, side):
    nz, ny, nx = fields[0].shape
    plane = pl.BlockSpec((1, ny, nx), lambda k: (k, 0, 0))
    fixed = pl.BlockSpec((ny, nx), lambda k: (0, 0))
    out_shape = [jax.ShapeDtypeStruct((nz, ny, nx), jnp.float32)] * 4
    return pl.pallas_call(
        _interior_kernel,
        grid=(nz,),
        in_specs=[fixed, fixed, plane, plane, plane, plane,
                  pl.BlockSpec((1, 4, RING_ROWS, RING_COLS), lambda k: (k, 0, 0, 0))],
        out_specs=[plane] * 4,
        out_shape=out_shape,
        scratch_shapes=[pltpu.VMEM((4, RING_ROWS, nx + RING_COLS), jnp.float32),
                        pltpu.VMEM((1, RING_ROWS, nx + RING_COLS), jnp.float32)],
        compiler_params=pltpu.CompilerParams(dimension_semantics=("arbitrary",)),
        cost_estimate=pl.CostEstimate(flops=200 * 4 * nz * ny * nx, transcendentals=0,
                                      bytes_accessed=8 * 4 * nz * ny * nx),
    )(levels, cor, *fields, side)


def _frame_kernel(levels_ref, cor_ref, t_ref, s_ref, u_ref, v_ref, north_ref, fold_ref, south_ref, side_ref,
                  at_ref, as_ref, au_ref, av_ref, ot_ref, os_ref, ou_ref, ov_ref, slab_ref, cum_ref):
    k = pl.program_id(0)
    half = pl.program_id(1)
    nx = t_ref.shape[2]

    @pl.when(k == 0)
    def _():
        cum_ref[half] = jnp.zeros(cum_ref.shape[1:], jnp.float32)

    wet = (levels_ref[...] > k).astype(jnp.float32)
    zeros2 = jnp.zeros((2, nx), jnp.float32)
    for c, ref in enumerate((t_ref, s_ref, u_ref, v_ref)):
        own = ref[0] * wet

        @pl.when(half == 0)
        def _():
            slab_ref[c, 0:4, 0:nx] = own[0:4]
            slab_ref[c, 4:6, 0:nx] = zeros2
            slab_ref[c, 6:8, 0:nx] = south_ref[0, c]

        @pl.when(half == 1)
        def _():
            for r in range(2):
                for b in range(nx // RING_COLS):
                    src_cols = slice(nx - (b + 1) * RING_COLS, nx - b * RING_COLS)
                    dst_cols = slice(b * RING_COLS, (b + 1) * RING_COLS)
                    slab_ref[c, r:r + 1, dst_cols] = (
                        north_ref[0, c, r:r + 1, dst_cols] + fold_ref[0, c, 1 - r:2 - r, src_cols])
            slab_ref[c, 2:4, 0:nx] = zeros2
            slab_ref[c, 4:8, 0:nx] = own[4:8]

        slab_ref[c, :, nx:] = side_ref[0, 0, c]
    results = _physics(slab_ref, cum_ref, half, cor_ref[...], wet, 8)
    row = lax.broadcasted_iota(jnp.int32, (8, nx), 0)
    first = half * 6
    keep = (row < first) | (row >= first + 2)
    for a_ref, o_ref, res in zip((at_ref, as_ref, au_ref, av_ref), (ot_ref, os_ref, ou_ref, ov_ref), results):
        o_ref[0] = jnp.where(keep, a_ref[0], res)


def frame_call(levels, cor, fields, north, fold, south, side, interior):
    nz, ny, nx = fields[0].shape
    tile = pl.BlockSpec((1, 8, nx), lambda k, h: (k, h, 0))
    fixed = pl.BlockSpec((8, nx), lambda k, h: (h, 0))
    rows = pl.BlockSpec((1, 4, 2, nx), lambda k, h: (k, 0, 0, 0))
    out_shape = [jax.ShapeDtypeStruct((nz, ny, nx), jnp.float32)] * 4
    return pl.pallas_call(
        _frame_kernel,
        grid=(nz, 2),
        in_specs=[fixed, fixed, tile, tile, tile, tile, rows, rows, rows,
                  pl.BlockSpec((1, 1, 4, 8, RING_COLS), lambda k, h: (k, h, 0, 0, 0)),
                  tile, tile, tile, tile],
        out_specs=[tile] * 4,
        out_shape=out_shape,
        input_output_aliases={10: 0, 11: 1, 12: 2, 13: 3},
        scratch_shapes=[pltpu.VMEM((4, 8, nx + RING_COLS), jnp.float32),
                        pltpu.VMEM((2, 8, nx + RING_COLS), jnp.float32)],
        compiler_params=pltpu.CompilerParams(dimension_semantics=("arbitrary", "arbitrary")),
    )(levels, cor, *fields, north, fold, south, side, *interior)


def pack_lanes(east, west):
    gap = jnp.zeros(east.shape[:-1] + (RING_COLS - 4,), jnp.float32)
    return jnp.concatenate([east, gap, west], axis=-1)


def pack_side(west, east, sw, nw, se, ne):
    nc, nz, ny, _ = west.shape
    zero = jnp.zeros((nc, nz), jnp.float32)
    gap = jnp.zeros((nc, nz, RING_ROWS - ny - 2, 2), jnp.float32)

    def block(cols, top, bottom):
        return jnp.concatenate([cols, top[:, :, None, :], gap, bottom[:, :, None, :]], axis=2)

    east_block = block(east, jnp.stack([ne, zero], -1), jnp.stack([se, zero], -1))
    west_block = block(west, jnp.stack([zero, nw], -1), jnp.stack([zero, sw], -1))
    side = jnp.concatenate(
        [east_block, jnp.zeros((nc, nz, RING_ROWS, RING_COLS - 4), jnp.float32), west_block], axis=3)
    return jnp.swapaxes(side, 0, 1)


def flip_lanes_in_blocks(x):
    *lead, n = x.shape
    lane = jnp.arange(128)
    anti = lax.optimization_barrier((lane[:, None] + lane[None, :] == 127).astype(jnp.float32))
    flipped = jnp.einsum("...i,ij->...j", x.reshape(*lead, n // 128, 128), anti,
                         precision=lax.Precision.HIGHEST)
    return flipped.reshape(*lead, n)


def shift_pairs(count, step, wrap):
    pairs = []
    for i in range(count):
        j = i + step
        if wrap:
            pairs.append((i, j % count))
        elif 0 <= j < count:
            pairs.append((i, j))
    return pairs


def per_device(
    thermal_anomaly,
    saltiness_anomaly,
    zonal_velocity_array,
    meridional_velocity_array,
    seawater_profile_flags,
    submerged_layer_total,
    computed_block_flags,
):
    raw = (thermal_anomaly, saltiness_anomaly, zonal_velocity_array, meridional_velocity_array)
    block_depth_layers = thermal_anomaly.shape[0]
    block_meridional_extent = thermal_anomaly.shape[1]
    n_lon = lax.axis_size("lon")
    n_lat = lax.axis_size("lat")
    tile_alive = computed_block_flags[0, 0] == 1
    levels = jnp.where((seawater_profile_flags == 1) & tile_alive, submerged_layer_total, 0)
    depth_index = jnp.arange(block_depth_layers, dtype=jnp.int32)[:, None, None]

    def masked(rows, cols):
        wet = (depth_index < levels[None, rows, cols]).astype(jnp.float32)
        return jnp.stack([f[:, rows, cols] for f in raw]) * wet

    every = slice(None)
    last = n_lat - 1
    both = ("lon", "lat")
    ny, nx = block_meridional_extent, thermal_anomaly.shape[2]
    nc = len(raw)
    west = lax.ppermute(masked(every, slice(-2, None)), "lon", shift_pairs(n_lon, 1, True))
    east = lax.ppermute(masked(every, slice(0, 2)), "lon", shift_pairs(n_lon, -1, True))
    top = masked(slice(-2, None), every)
    folded = lax.ppermute(top, both, [(p * n_lat + last, (n_lon - 1 - p) * n_lat + last) for p in range(n_lon)])
    bottom = masked(slice(0, 2), every)
    from_south = lax.ppermute(top, "lat", shift_pairs(n_lat, 1, False))
    from_north = lax.ppermute(bottom, "lat", shift_pairs(n_lat, -1, False))
    signs = jnp.array([1.0, 1.0, -1.0, -1.0], jnp.float32).reshape(4, 1, 1, 1)
    is_northern = lax.axis_index("lat") == last

    def north_cols(cols):
        fold_part = jnp.stack(
            [jnp.stack([folded[:, :, 1 - r, nx - 1 - i] for i in cols], axis=-1) for r in range(2)], axis=2)
        return jnp.where(is_northern, fold_part * signs, from_north[..., cols[0]:cols[-1] + 1])

    halo_west = lax.ppermute(
        jnp.concatenate([from_south[..., -2:], north_cols((nx - 2, nx - 1))], axis=2),
        "lon", shift_pairs(n_lon, 1, True))
    halo_east = lax.ppermute(
        jnp.concatenate([from_south[..., :2], north_cols((0, 1))], axis=2),
        "lon", shift_pairs(n_lon, -1, True))
    zero_rows = jnp.zeros((nc, block_depth_layers, RING_ROWS - ny, RING_COLS), jnp.float32)
    side_interior = jnp.concatenate([pack_lanes(east, west), zero_rows], axis=2)
    gap = jnp.zeros((nc, block_depth_layers, 2, 2), jnp.float32)
    lower = pack_lanes(jnp.concatenate([east[:, :, 0:4], gap, halo_east[:, :, 0:2]], axis=2),
                       jnp.concatenate([west[:, :, 0:4], gap, halo_west[:, :, 0:2]], axis=2))
    upper = pack_lanes(jnp.concatenate([halo_east[:, :, 2:4], gap, east[:, :, ny - 4:]], axis=2),
                       jnp.concatenate([halo_west[:, :, 2:4], gap, west[:, :, ny - 4:]], axis=2))
    side_frame = jnp.stack([lower, upper], axis=0).transpose(2, 0, 1, 3, 4)
    fold_rows = flip_lanes_in_blocks(folded) * signs
    total_rows = block_meridional_extent * n_lat
    row_pos = (
        lax.axis_index("lat") * block_meridional_extent
        + jnp.arange(block_meridional_extent, dtype=jnp.int32)
    ).astype(jnp.float32)
    coriolis = (CORIOLIS_MAX * jnp.sin(jnp.pi * ((row_pos + 0.5) / total_rows - 0.5)))[:, None]
    cor = jnp.broadcast_to(coriolis, levels.shape)
    interior = interior_call(levels, cor, raw, jnp.swapaxes(side_interior, 0, 1))
    return tuple(frame_call(levels, cor, raw, jnp.swapaxes(from_north, 0, 1), jnp.swapaxes(fold_rows, 0, 1),
                            jnp.swapaxes(from_south, 0, 1), side_frame, interior))


def solution(mesh):
    return jax.shard_map(
        per_device,
        mesh=mesh,
        in_specs=(
            P(None, "lat", "lon"),
            P(None, "lat", "lon"),
            P(None, "lat", "lon"),
            P(None, "lat", "lon"),
            P("lat", "lon"),
            P("lat", "lon"),
            P("lat", "lon"),
        ),
        out_specs=(
            P(None, "lat", "lon"),
            P(None, "lat", "lon"),
            P(None, "lat", "lon"),
            P(None, "lat", "lon"),
        ),
        check_vma=False,
    )
```

```python
import jax
import jax.numpy as jnp
from jax import lax
from jax.sharding import PartitionSpec as P
from jax.experimental import pallas as pl
from jax.experimental.pallas import tpu as pltpu


ALPHA = 0.2
BETA = 0.8
GRAV_DZ = 0.1
DT_STEP = 0.2
VISC_TWO = 0.1
VISC_FOUR = 0.05
CORIOLIS_MAX = 0.3


def with_halo(value, sides, width, wrap):
    for axis, dim in sides:
        count, length = (lax.axis_size(axis), value.shape[dim])
        up = [(i, (i + 1) % count) for i in range(count if wrap else count - 1)]
        down = [(j, i) for i, j in up]
        last = lax.slice_in_dim(value, length - width, length, axis=dim)
        first = lax.slice_in_dim(value, 0, width, axis=dim)
        before = lax.ppermute(last, axis, up)
        after = lax.ppermute(first, axis, down)
        value = jnp.concatenate([before, value, after], axis=dim)
    return value


def from_partner(value, axis, distance):
    mask = 2**distance
    pairs = [(source, source ^ mask) for source in range(lax.axis_size(axis))]
    return lax.ppermute(value, axis, pairs)


def laplace(field):
    return (
        field[..., 2:, 1:-1]
        + field[..., :-2, 1:-1]
        + field[..., 1:-1, 2:]
        + field[..., 1:-1, :-2]
        - 4.0 * field[..., 1:-1, 1:-1]
    )


def update_fields(extended, submerged_share, coriolis):
    temper = extended[0]
    saline = extended[1]
    eastward = extended[2]
    northward = extended[3]
    density = BETA * saline - ALPHA * temper
    pressure = GRAV_DZ * (jnp.cumsum(density, axis=0) - 0.5 * density)
    laplacian = laplace(extended)
    bilaplacian = laplace(laplacian)
    centre = extended[..., 2:-2, 2:-2]
    mixing = VISC_TWO * laplacian[..., 1:-1, 1:-1] - VISC_FOUR * bilaplacian
    grad_east = 0.5 * (pressure[:, 2:-2, 3:-1] - pressure[:, 2:-2, 1:-3])
    grad_north = 0.5 * (pressure[:, 3:-1, 2:-2] - pressure[:, 1:-3, 2:-2])
    tracers = extended[0:2]
    flux_east = tracers * eastward
    flux_north = tracers * northward
    advection = 0.5 * (flux_east[..., 2:-2, 3:-1] - flux_east[..., 2:-2, 1:-3]) + 0.5 * (
        flux_north[..., 3:-1, 2:-2] - flux_north[..., 1:-3, 2:-2]
    )
    accel_east = coriolis * centre[3] - grad_east
    accel_north = -coriolis * centre[2] - grad_north
    forcing = jnp.concatenate([-advection, accel_east[None], accel_north[None]], axis=0)
    return submerged_share * (centre + DT_STEP * (forcing + mixing))


RING_ROWS = 24
RING_COLS = 128


def _lap(a):
    rows, cols = a.shape
    return (
        pltpu.roll(a, rows - 1, 0)
        + pltpu.roll(a, 1, 0)
        + pltpu.roll(a, cols - 1, 1)
        + pltpu.roll(a, 1, 1)
        - 4.0 * a
    )


def _physics(ext_ref, cum_ref, which, cor, wet, rows):
    nx = ext_ref.shape[2] - RING_COLS

    def centre(a):
        return a[0:rows, 0:nx]

    def east(a):
        return centre(pltpu.roll(a, a.shape[1] - 1, 1))

    def west(a):
        return centre(pltpu.roll(a, 1, 1))

    def north(a):
        return centre(pltpu.roll(a, a.shape[0] - 1, 0))

    def south(a):
        return centre(pltpu.roll(a, 1, 0))

    temper = ext_ref[0]
    saline = ext_ref[1]
    density = BETA * saline - ALPHA * temper
    cum = cum_ref[which] + density
    cum_ref[which] = cum
    pressure = GRAV_DZ * (cum - 0.5 * density)
    grad_east = 0.5 * (east(pressure) - west(pressure))
    grad_north = 0.5 * (north(pressure) - south(pressure))
    eastward = ext_ref[2]
    northward = ext_ref[3]
    results = []
    for c in range(4):
        field = ext_ref[c]
        lap = _lap(field)
        bil = (north(lap) + south(lap) + east(lap) + west(lap) - 4.0 * centre(lap))
        mixing = VISC_TWO * centre(lap) - VISC_FOUR * bil
        if c < 2:
            fe = field * eastward
            fn = field * northward
            adv = 0.5 * (east(fe) - west(fe)) + 0.5 * (north(fn) - south(fn))
            forcing = -adv
        elif c == 2:
            forcing = cor * centre(northward) - grad_east
        else:
            forcing = -cor * centre(eastward) - grad_north
        results.append(wet * (centre(field) + DT_STEP * (forcing + mixing)))
    return results


def _interior_kernel(levels_ref, cor_ref, t_ref, s_ref, u_ref, v_ref, side_ref,
                     ot_ref, os_ref, ou_ref, ov_ref, ext_ref, cum_ref):
    k = pl.program_id(0)
    ny, nx = t_ref.shape[1], t_ref.shape[2]

    @pl.when(k == 0)
    def _():
        cum_ref[...] = jnp.zeros_like(cum_ref)
        ext_ref[...] = jnp.zeros_like(ext_ref)

    wet = (levels_ref[...] > k).astype(jnp.float32)
    for c, ref in enumerate((t_ref, s_ref, u_ref, v_ref)):
        ext_ref[c, 0:ny, 0:nx] = ref[0] * wet
        ext_ref[c, :, nx:] = side_ref[0, c]
    results = _physics(ext_ref, cum_ref, 0, cor_ref[...], wet, ny)
    for o, res in zip((ot_ref, os_ref, ou_ref, ov_ref), results):
        o[0] = res


def interior_call(levels, cor, fields, side):
    nz, ny, nx = fields[0].shape
    plane = pl.BlockSpec((1, ny, nx), lambda k: (k, 0, 0))
    fixed = pl.BlockSpec((ny, nx), lambda k: (0, 0))
    out_shape = [jax.ShapeDtypeStruct((nz, ny, nx), jnp.float32)] * 4
    return pl.pallas_call(
        _interior_kernel,
        grid=(nz,),
        in_specs=[fixed, fixed, plane, plane, plane, plane,
                  pl.BlockSpec((1, 4, RING_ROWS, RING_COLS), lambda k: (k, 0, 0, 0))],
        out_specs=[plane] * 4,
        out_shape=out_shape,
        scratch_shapes=[pltpu.VMEM((4, RING_ROWS, nx + RING_COLS), jnp.float32),
                        pltpu.VMEM((1, RING_ROWS, nx + RING_COLS), jnp.float32)],
        compiler_params=pltpu.CompilerParams(dimension_semantics=("arbitrary",)),
        cost_estimate=pl.CostEstimate(flops=200 * 4 * nz * ny * nx, transcendentals=0,
                                      bytes_accessed=8 * 4 * nz * ny * nx),
    )(levels, cor, *fields, side)


FRAME_LEVELS = 5


def _frame_kernel(levels_ref, cor_ref, t_ref, s_ref, u_ref, v_ref, north_ref, fold_ref, south_ref, side_ref,
                  at_ref, as_ref, au_ref, av_ref, ot_ref, os_ref, ou_ref, ov_ref, slab_ref, cum_ref):
    step = pl.program_id(0)
    per_step, ny, nx = t_ref.shape

    @pl.when(step == 0)
    def _():
        cum_ref[...] = jnp.zeros_like(cum_ref)

    row = lax.broadcasted_iota(jnp.int32, (8, nx), 0)
    zeros2 = jnp.zeros((2, nx), jnp.float32)
    ins = (t_ref, s_ref, u_ref, v_ref)
    prev = (at_ref, as_ref, au_ref, av_ref)
    outs = (ot_ref, os_ref, ou_ref, ov_ref)

    def level(l, carry):
        k = step * per_step + l
        wet = (levels_ref[...] > k).astype(jnp.float32)
        for c, ref in enumerate(ins):
            slab_ref[c, 0:4, 0:nx] = ref[l, 0:4] * wet[0:4]
            slab_ref[c, 4:6, 0:nx] = zeros2
            slab_ref[c, 6:8, 0:nx] = south_ref[l, c]
            slab_ref[c, :, nx:] = side_ref[l, 0, c]
        lower = _physics(slab_ref, cum_ref, 0, cor_ref[0:8], wet[0:8], 8)
        for c in range(4):
            outs[c][l, 0:8] = jnp.where(row < 2, lower[c], prev[c][l, 0:8])
        for c, ref in enumerate(ins):
            for r in range(2):
                for b in range(nx // RING_COLS):
                    src_cols = slice(nx - (b + 1) * RING_COLS, nx - b * RING_COLS)
                    dst_cols = slice(b * RING_COLS, (b + 1) * RING_COLS)
                    slab_ref[c, r:r + 1, dst_cols] = (
                        north_ref[l, c, r:r + 1, dst_cols] + fold_ref[l, c, 1 - r:2 - r, src_cols])
            slab_ref[c, 2:4, 0:nx] = zeros2
            slab_ref[c, 4:8, 0:nx] = ref[l, ny - 4:ny] * wet[ny - 4:ny]
            slab_ref[c, :, nx:] = side_ref[l, 1, c]
        upper = _physics(slab_ref, cum_ref, 1, cor_ref[ny - 8:ny], wet[ny - 8:ny], 8)
        for c in range(4):
            outs[c][l, ny - 8:ny] = jnp.where(row >= 6, upper[c], prev[c][l, ny - 8:ny])
        return carry

    lax.fori_loop(0, per_step, level, 0)


def frame_call(levels, cor, fields, north, fold, south, side, interior):
    nz, ny, nx = fields[0].shape
    per = FRAME_LEVELS if nz % FRAME_LEVELS == 0 else 1
    plane = pl.BlockSpec((per, ny, nx), lambda k: (k, 0, 0))
    fixed = pl.BlockSpec((ny, nx), lambda k: (0, 0))
    rows = pl.BlockSpec((per, 4, 2, nx), lambda k: (k, 0, 0, 0))
    out_shape = [jax.ShapeDtypeStruct((nz, ny, nx), jnp.float32)] * 4
    return pl.pallas_call(
        _frame_kernel,
        grid=(nz // per,),
        in_specs=[fixed, fixed, plane, plane, plane, plane, rows, rows, rows,
                  pl.BlockSpec((per, 2, 4, 8, RING_COLS), lambda k: (k, 0, 0, 0, 0)),
                  plane, plane, plane, plane],
        out_specs=[plane] * 4,
        out_shape=out_shape,
        input_output_aliases={10: 0, 11: 1, 12: 2, 13: 3},
        scratch_shapes=[pltpu.VMEM((4, 8, nx + RING_COLS), jnp.float32),
                        pltpu.VMEM((2, 8, nx + RING_COLS), jnp.float32)],
        compiler_params=pltpu.CompilerParams(dimension_semantics=("arbitrary",)),
    )(levels, cor, *fields, north, fold, south, side, *interior)


def pack_lanes(east, west):
    gap = jnp.zeros(east.shape[:-1] + (RING_COLS - 4,), jnp.float32)
    return jnp.concatenate([east, gap, west], axis=-1)


def pack_side(west, east, sw, nw, se, ne):
    nc, nz, ny, _ = west.shape
    zero = jnp.zeros((nc, nz), jnp.float32)
    gap = jnp.zeros((nc, nz, RING_ROWS - ny - 2, 2), jnp.float32)

    def block(cols, top, bottom):
        return jnp.concatenate([cols, top[:, :, None, :], gap, bottom[:, :, None, :]], axis=2)

    east_block = block(east, jnp.stack([ne, zero], -1), jnp.stack([se, zero], -1))
    west_block = block(west, jnp.stack([zero, nw], -1), jnp.stack([zero, sw], -1))
    side = jnp.concatenate(
        [east_block, jnp.zeros((nc, nz, RING_ROWS, RING_COLS - 4), jnp.float32), west_block], axis=3)
    return jnp.swapaxes(side, 0, 1)


def flip_lanes_in_blocks(x):
    *lead, n = x.shape
    lane = jnp.arange(128)
    anti = lax.optimization_barrier((lane[:, None] + lane[None, :] == 127).astype(jnp.float32))
    flipped = jnp.einsum("...i,ij->...j", x.reshape(*lead, n // 128, 128), anti,
                         precision=lax.Precision.HIGHEST)
    return flipped.reshape(*lead, n)


def shift_pairs(count, step, wrap):
    pairs = []
    for i in range(count):
        j = i + step
        if wrap:
            pairs.append((i, j % count))
        elif 0 <= j < count:
            pairs.append((i, j))
    return pairs


def per_device(
    thermal_anomaly,
    saltiness_anomaly,
    zonal_velocity_array,
    meridional_velocity_array,
    seawater_profile_flags,
    submerged_layer_total,
    computed_block_flags,
):
    raw = (thermal_anomaly, saltiness_anomaly, zonal_velocity_array, meridional_velocity_array)
    block_depth_layers = thermal_anomaly.shape[0]
    block_meridional_extent = thermal_anomaly.shape[1]
    n_lon = lax.axis_size("lon")
    n_lat = lax.axis_size("lat")
    tile_alive = computed_block_flags[0, 0] == 1
    levels = jnp.where((seawater_profile_flags == 1) & tile_alive, submerged_layer_total, 0)
    depth_index = jnp.arange(block_depth_layers, dtype=jnp.int32)[:, None, None]

    def masked(rows, cols):
        wet = (depth_index < levels[None, rows, cols]).astype(jnp.float32)
        return jnp.stack([f[:, rows, cols] for f in raw]) * wet

    every = slice(None)
    last = n_lat - 1
    both = ("lon", "lat")
    ny, nx = block_meridional_extent, thermal_anomaly.shape[2]
    nc = len(raw)
    top = masked(slice(-2, None), every)
    folded = lax.ppermute(top, both, [(p * n_lat + last, (n_lon - 1 - p) * n_lat + last) for p in range(n_lon)])
    west = lax.ppermute(masked(every, slice(-2, None)), "lon", shift_pairs(n_lon, 1, True))
    east = lax.ppermute(masked(every, slice(0, 2)), "lon", shift_pairs(n_lon, -1, True))
    bottom = masked(slice(0, 2), every)
    from_south = lax.ppermute(top, "lat", shift_pairs(n_lat, 1, False))
    from_north = lax.ppermute(bottom, "lat", shift_pairs(n_lat, -1, False))
    signs = jnp.array([1.0, 1.0, -1.0, -1.0], jnp.float32).reshape(4, 1, 1, 1)
    is_northern = lax.axis_index("lat") == last

    def north_cols(cols):
        fold_part = jnp.stack(
            [jnp.stack([folded[:, :, 1 - r, nx - 1 - i] for i in cols], axis=-1) for r in range(2)], axis=2)
        return jnp.where(is_northern, fold_part * signs, from_north[..., cols[0]:cols[-1] + 1])

    halo_west = lax.ppermute(
        jnp.concatenate([from_south[..., -2:], north_cols((nx - 2, nx - 1))], axis=2),
        "lon", shift_pairs(n_lon, 1, True))
    halo_east = lax.ppermute(
        jnp.concatenate([from_south[..., :2], north_cols((0, 1))], axis=2),
        "lon", shift_pairs(n_lon, -1, True))
    zero_rows = jnp.zeros((nc, block_depth_layers, RING_ROWS - ny, RING_COLS), jnp.float32)
    side_interior = jnp.concatenate([pack_lanes(east, west), zero_rows], axis=2)
    gap = jnp.zeros((nc, block_depth_layers, 2, 2), jnp.float32)
    lower = pack_lanes(jnp.concatenate([east[:, :, 0:4], gap, halo_east[:, :, 0:2]], axis=2),
                       jnp.concatenate([west[:, :, 0:4], gap, halo_west[:, :, 0:2]], axis=2))
    upper = pack_lanes(jnp.concatenate([halo_east[:, :, 2:4], gap, east[:, :, ny - 4:]], axis=2),
                       jnp.concatenate([halo_west[:, :, 2:4], gap, west[:, :, ny - 4:]], axis=2))
    side_frame = jnp.stack([lower, upper], axis=0).transpose(2, 0, 1, 3, 4)
    fold_rows = flip_lanes_in_blocks(folded) * signs
    total_rows = block_meridional_extent * n_lat
    row_pos = (
        lax.axis_index("lat") * block_meridional_extent
        + jnp.arange(block_meridional_extent, dtype=jnp.int32)
    ).astype(jnp.float32)
    coriolis = (CORIOLIS_MAX * jnp.sin(jnp.pi * ((row_pos + 0.5) / total_rows - 0.5)))[:, None]
    cor = jnp.broadcast_to(coriolis, levels.shape)
    interior = interior_call(levels, cor, raw, jnp.swapaxes(side_interior, 0, 1))
    return tuple(frame_call(levels, cor, raw, jnp.swapaxes(from_north, 0, 1), jnp.swapaxes(fold_rows, 0, 1),
                            jnp.swapaxes(from_south, 0, 1), side_frame, interior))


def solution(mesh):
    return jax.shard_map(
        per_device,
        mesh=mesh,
        in_specs=(
            P(None, "lat", "lon"),
            P(None, "lat", "lon"),
            P(None, "lat", "lon"),
            P(None, "lat", "lon"),
            P("lat", "lon"),
            P("lat", "lon"),
            P("lat", "lon"),
        ),
        out_specs=(
            P(None, "lat", "lon"),
            P(None, "lat", "lon"),
            P(None, "lat", "lon"),
            P(None, "lat", "lon"),
        ),
        check_vma=False,
    )
```

```python
import jax
import jax.numpy as jnp
from jax import lax
from jax.sharding import PartitionSpec as P
from jax.experimental import pallas as pl
from jax.experimental.pallas import tpu as pltpu


ALPHA = 0.2
BETA = 0.8
GRAV_DZ = 0.1
DT_STEP = 0.2
VISC_TWO = 0.1
VISC_FOUR = 0.05
CORIOLIS_MAX = 0.3


def with_halo(value, sides, width, wrap):
    for axis, dim in sides:
        count, length = (lax.axis_size(axis), value.shape[dim])
        up = [(i, (i + 1) % count) for i in range(count if wrap else count - 1)]
        down = [(j, i) for i, j in up]
        last = lax.slice_in_dim(value, length - width, length, axis=dim)
        first = lax.slice_in_dim(value, 0, width, axis=dim)
        before = lax.ppermute(last, axis, up)
        after = lax.ppermute(first, axis, down)
        value = jnp.concatenate([before, value, after], axis=dim)
    return value


def from_partner(value, axis, distance):
    mask = 2**distance
    pairs = [(source, source ^ mask) for source in range(lax.axis_size(axis))]
    return lax.ppermute(value, axis, pairs)


def laplace(field):
    return (
        field[..., 2:, 1:-1]
        + field[..., :-2, 1:-1]
        + field[..., 1:-1, 2:]
        + field[..., 1:-1, :-2]
        - 4.0 * field[..., 1:-1, 1:-1]
    )


def update_fields(extended, submerged_share, coriolis):
    temper = extended[0]
    saline = extended[1]
    eastward = extended[2]
    northward = extended[3]
    density = BETA * saline - ALPHA * temper
    pressure = GRAV_DZ * (jnp.cumsum(density, axis=0) - 0.5 * density)
    laplacian = laplace(extended)
    bilaplacian = laplace(laplacian)
    centre = extended[..., 2:-2, 2:-2]
    mixing = VISC_TWO * laplacian[..., 1:-1, 1:-1] - VISC_FOUR * bilaplacian
    grad_east = 0.5 * (pressure[:, 2:-2, 3:-1] - pressure[:, 2:-2, 1:-3])
    grad_north = 0.5 * (pressure[:, 3:-1, 2:-2] - pressure[:, 1:-3, 2:-2])
    tracers = extended[0:2]
    flux_east = tracers * eastward
    flux_north = tracers * northward
    advection = 0.5 * (flux_east[..., 2:-2, 3:-1] - flux_east[..., 2:-2, 1:-3]) + 0.5 * (
        flux_north[..., 3:-1, 2:-2] - flux_north[..., 1:-3, 2:-2]
    )
    accel_east = coriolis * centre[3] - grad_east
    accel_north = -coriolis * centre[2] - grad_north
    forcing = jnp.concatenate([-advection, accel_east[None], accel_north[None]], axis=0)
    return submerged_share * (centre + DT_STEP * (forcing + mixing))


RING_ROWS = 24
RING_COLS = 128


def _lap(a):
    rows, cols = a.shape
    return (
        pltpu.roll(a, rows - 1, 0)
        + pltpu.roll(a, 1, 0)
        + pltpu.roll(a, cols - 1, 1)
        + pltpu.roll(a, 1, 1)
        - 4.0 * a
    )


def _step_kernel(levels_ref, cor_ref, t_ref, s_ref, u_ref, v_ref, north_ref, fold_ref, south_ref, side_ref,
                 ot_ref, os_ref, ou_ref, ov_ref, ext_ref, cum_ref):
    k = pl.program_id(0)
    ny, nx = t_ref.shape[1], t_ref.shape[2]

    @pl.when(k == 0)
    def _():
        cum_ref[...] = jnp.zeros_like(cum_ref)
        ext_ref[...] = jnp.zeros_like(ext_ref)

    wet = (levels_ref[...] > k).astype(jnp.float32)
    for c, ref in enumerate((t_ref, s_ref, u_ref, v_ref)):
        ext_ref[c, 0:ny, 0:nx] = ref[0] * wet
        for r in range(2):
            for b in range(nx // RING_COLS):
                src_cols = slice(nx - (b + 1) * RING_COLS, nx - b * RING_COLS)
                dst_cols = slice(b * RING_COLS, (b + 1) * RING_COLS)
                ext_ref[c, ny + r:ny + r + 1, dst_cols] = (
                    north_ref[0, c, r:r + 1, dst_cols] + fold_ref[0, c, 1 - r:2 - r, src_cols])
        ext_ref[c, RING_ROWS - 2:RING_ROWS, 0:nx] = south_ref[0, c]
        ext_ref[c, :, nx:] = side_ref[0, c]

    def centre(a):
        return a[0:ny, 0:nx]

    def east(a):
        return centre(pltpu.roll(a, a.shape[1] - 1, 1))

    def west(a):
        return centre(pltpu.roll(a, 1, 1))

    def north(a):
        return centre(pltpu.roll(a, a.shape[0] - 1, 0))

    def south(a):
        return centre(pltpu.roll(a, 1, 0))

    temper = ext_ref[0]
    saline = ext_ref[1]
    density = BETA * saline - ALPHA * temper
    cum = cum_ref[...] + density
    cum_ref[...] = cum
    pressure = GRAV_DZ * (cum - 0.5 * density)
    grad_east = 0.5 * (east(pressure) - west(pressure))
    grad_north = 0.5 * (north(pressure) - south(pressure))
    eastward = ext_ref[2]
    northward = ext_ref[3]
    cor = cor_ref[...]
    outs = (ot_ref, os_ref, ou_ref, ov_ref)
    for c in range(4):
        field = ext_ref[c]
        lap = _lap(field)
        bil = (north(lap) + south(lap) + east(lap) + west(lap) - 4.0 * centre(lap))
        mixing = VISC_TWO * centre(lap) - VISC_FOUR * bil
        if c < 2:
            fe = field * eastward
            fn = field * northward
            adv = 0.5 * (east(fe) - west(fe)) + 0.5 * (north(fn) - south(fn))
            forcing = -adv
        elif c == 2:
            forcing = cor * centre(northward) - grad_east
        else:
            forcing = -cor * centre(eastward) - grad_north
        outs[c][0] = wet * (centre(field) + DT_STEP * (forcing + mixing))


def stencil_call(levels, cor, fields, north, fold, south, side):
    nz, ny, nx = fields[0].shape
    plane = pl.BlockSpec((1, ny, nx), lambda k: (k, 0, 0))
    fixed = pl.BlockSpec((ny, nx), lambda k: (0, 0))
    rows = pl.BlockSpec((1, 4, 2, nx), lambda k: (k, 0, 0, 0))
    out_shape = [jax.ShapeDtypeStruct((nz, ny, nx), jnp.float32)] * 4
    return pl.pallas_call(
        _step_kernel,
        grid=(nz,),
        in_specs=[fixed, fixed, plane, plane, plane, plane, rows, rows, rows,
                  pl.BlockSpec((1, 4, RING_ROWS, RING_COLS), lambda k: (k, 0, 0, 0))],
        out_specs=[plane] * 4,
        out_shape=out_shape,
        scratch_shapes=[pltpu.VMEM((4, RING_ROWS, nx + RING_COLS), jnp.float32),
                        pltpu.VMEM((RING_ROWS, nx + RING_COLS), jnp.float32)],
        compiler_params=pltpu.CompilerParams(dimension_semantics=("arbitrary",)),
    )(levels, cor, *fields, north, fold, south, side)


def pack_side(west, east, sw, nw, se, ne):
    nc, nz, ny, _ = west.shape
    zero = jnp.zeros((nc, nz), jnp.float32)
    gap = jnp.zeros((nc, nz, RING_ROWS - ny - 2, 2), jnp.float32)

    def block(cols, top, bottom):
        return jnp.concatenate([cols, top[:, :, None, :], gap, bottom[:, :, None, :]], axis=2)

    east_block = block(east, jnp.stack([ne, zero], -1), jnp.stack([se, zero], -1))
    west_block = block(west, jnp.stack([zero, nw], -1), jnp.stack([zero, sw], -1))
    side = jnp.concatenate(
        [east_block, jnp.zeros((nc, nz, RING_ROWS, RING_COLS - 4), jnp.float32), west_block], axis=3)
    return jnp.swapaxes(side, 0, 1)


def flip_lanes_in_blocks(x):
    *lead, n = x.shape
    lane = jnp.arange(128)
    anti = lax.optimization_barrier((lane[:, None] + lane[None, :] == 127).astype(jnp.float32))
    flipped = jnp.einsum("...i,ij->...j", x.reshape(*lead, n // 128, 128), anti,
                         precision=lax.Precision.HIGHEST)
    return flipped.reshape(*lead, n)


def shift_pairs(count, step, wrap):
    pairs = []
    for i in range(count):
        j = i + step
        if wrap:
            pairs.append((i, j % count))
        elif 0 <= j < count:
            pairs.append((i, j))
    return pairs


def per_device(
    thermal_anomaly,
    saltiness_anomaly,
    zonal_velocity_array,
    meridional_velocity_array,
    seawater_profile_flags,
    submerged_layer_total,
    computed_block_flags,
):
    raw = (thermal_anomaly, saltiness_anomaly, zonal_velocity_array, meridional_velocity_array)
    block_depth_layers = thermal_anomaly.shape[0]
    block_meridional_extent = thermal_anomaly.shape[1]
    n_lon = lax.axis_size("lon")
    n_lat = lax.axis_size("lat")
    tile_alive = computed_block_flags[0, 0] == 1
    levels = jnp.where((seawater_profile_flags == 1) & tile_alive, submerged_layer_total, 0)
    depth_index = jnp.arange(block_depth_layers, dtype=jnp.int32)[:, None, None]

    def masked(rows, cols):
        wet = (depth_index < levels[None, rows, cols]).astype(jnp.float32)
        return jnp.stack([f[:, rows, cols] for f in raw]) * wet

    every = slice(None)
    last = n_lat - 1
    both = ("lon", "lat")
    ny, nx = block_meridional_extent, thermal_anomaly.shape[2]
    top = masked(slice(-2, None), every)
    folded = lax.ppermute(top, both, [(p * n_lat + last, (n_lon - 1 - p) * n_lat + last) for p in range(n_lon)])
    bottom = masked(slice(0, 2), every)
    from_south = lax.ppermute(top, "lat", shift_pairs(n_lat, 1, False))
    from_north = lax.ppermute(bottom, "lat", shift_pairs(n_lat, -1, False))
    signs = jnp.array([1.0, 1.0, -1.0, -1.0], jnp.float32).reshape(4, 1, 1, 1)
    is_northern = lax.axis_index("lat") == last

    def north_cols(cols):
        fold_part = jnp.stack(
            [jnp.stack([folded[:, :, 1 - r, nx - 1 - i] for i in cols], axis=-1) for r in range(2)], axis=2)
        return jnp.where(is_northern, fold_part * signs, from_north[..., cols[0]:cols[-1] + 1])

    def tall(cols):
        return jnp.concatenate(
            [from_south[..., cols[0]:cols[-1] + 1], masked(every, slice(cols[0], cols[-1] + 1)), north_cols(cols)],
            axis=2)

    west = lax.ppermute(tall((nx - 2, nx - 1)), "lon", shift_pairs(n_lon, 1, True))
    east = lax.ppermute(tall((0, 1)), "lon", shift_pairs(n_lon, -1, True))
    side = pack_side(west[:, :, 2:-2], east[:, :, 2:-2], west[:, :, 1, 1], west[:, :, -2, 1],
                     east[:, :, 1, 0], east[:, :, -2, 0])
    fold_rows = flip_lanes_in_blocks(folded) * signs
    total_rows = block_meridional_extent * n_lat
    row_pos = (
        lax.axis_index("lat") * block_meridional_extent
        + jnp.arange(block_meridional_extent, dtype=jnp.int32)
    ).astype(jnp.float32)
    coriolis = (CORIOLIS_MAX * jnp.sin(jnp.pi * ((row_pos + 0.5) / total_rows - 0.5)))[:, None]
    cor = jnp.broadcast_to(coriolis, levels.shape)
    return tuple(stencil_call(levels, cor, raw, jnp.swapaxes(from_north, 0, 1), jnp.swapaxes(fold_rows, 0, 1),
                              jnp.swapaxes(from_south, 0, 1), side))


def solution(mesh):
    return jax.shard_map(
        per_device,
        mesh=mesh,
        in_specs=(
            P(None, "lat", "lon"),
            P(None, "lat", "lon"),
            P(None, "lat", "lon"),
            P(None, "lat", "lon"),
            P("lat", "lon"),
            P("lat", "lon"),
            P("lat", "lon"),
        ),
        out_specs=(
            P(None, "lat", "lon"),
            P(None, "lat", "lon"),
            P(None, "lat", "lon"),
            P(None, "lat", "lon"),
        ),
        check_vma=False,
    )
```

```python
import jax
import jax.numpy as jnp
from jax import lax
from jax.sharding import PartitionSpec as P
from jax.experimental import pallas as pl
from jax.experimental.pallas import tpu as pltpu


ALPHA = 0.2
BETA = 0.8
GRAV_DZ = 0.1
DT_STEP = 0.2
VISC_TWO = 0.1
VISC_FOUR = 0.05
CORIOLIS_MAX = 0.3


RING_ROWS = 24
RING_COLS = 128


def _lap(a):
    rows, cols = a.shape
    return (
        pltpu.roll(a, rows - 1, 0)
        + pltpu.roll(a, 1, 0)
        + pltpu.roll(a, cols - 1, 1)
        + pltpu.roll(a, 1, 1)
        - 4.0 * a
    )


def _step_kernel(levels_ref, cor_ref, t_ref, s_ref, u_ref, v_ref, north_ref, fold_ref, south_ref, side_ref,
                 ot_ref, os_ref, ou_ref, ov_ref, ext_ref, cum_ref):
    k = pl.program_id(0)
    ny, nx = t_ref.shape[1], t_ref.shape[2]

    @pl.when(k == 0)
    def _():
        cum_ref[...] = jnp.zeros_like(cum_ref)
        ext_ref[...] = jnp.zeros_like(ext_ref)

    wet = (levels_ref[...] > k).astype(jnp.float32)
    for c, ref in enumerate((t_ref, s_ref, u_ref, v_ref)):
        ext_ref[c, 0:ny, 0:nx] = ref[0] * wet
        for r in range(2):
            for b in range(nx // RING_COLS):
                src_cols = slice(nx - (b + 1) * RING_COLS, nx - b * RING_COLS)
                dst_cols = slice(b * RING_COLS, (b + 1) * RING_COLS)
                ext_ref[c, ny + r:ny + r + 1, dst_cols] = (
                    north_ref[0, c, r:r + 1, dst_cols] + fold_ref[0, c, 1 - r:2 - r, src_cols])
        ext_ref[c, RING_ROWS - 2:RING_ROWS, 0:nx] = south_ref[0, c]
        ext_ref[c, :, nx:] = side_ref[0, c]

    def centre(a):
        return a[0:ny, 0:nx]

    def east(a):
        return centre(pltpu.roll(a, a.shape[1] - 1, 1))

    def west(a):
        return centre(pltpu.roll(a, 1, 1))

    def north(a):
        return centre(pltpu.roll(a, a.shape[0] - 1, 0))

    def south(a):
        return centre(pltpu.roll(a, 1, 0))

    temper = ext_ref[0]
    saline = ext_ref[1]
    density = BETA * saline - ALPHA * temper
    cum = cum_ref[...] + density
    cum_ref[...] = cum
    pressure = GRAV_DZ * (cum - 0.5 * density)
    grad_east = 0.5 * (east(pressure) - west(pressure))
    grad_north = 0.5 * (north(pressure) - south(pressure))
    eastward = ext_ref[2]
    northward = ext_ref[3]
    cor = jnp.concatenate([cor_ref[...]] * (nx // RING_COLS), axis=1)
    outs = (ot_ref, os_ref, ou_ref, ov_ref)
    for c in range(4):
        field = ext_ref[c]
        lap = _lap(field)
        bil = (north(lap) + south(lap) + east(lap) + west(lap) - 4.0 * centre(lap))
        mixing = VISC_TWO * centre(lap) - VISC_FOUR * bil
        if c < 2:
            fe = field * eastward
            fn = field * northward
            adv = 0.5 * (east(fe) - west(fe)) + 0.5 * (north(fn) - south(fn))
            forcing = -adv
        elif c == 2:
            forcing = cor * centre(northward) - grad_east
        else:
            forcing = -cor * centre(eastward) - grad_north
        outs[c][0] = wet * (centre(field) + DT_STEP * (forcing + mixing))


def stencil_call(levels, cor, fields, north, fold, south, side):
    nz, ny, nx = fields[0].shape
    plane = pl.BlockSpec((1, ny, nx), lambda k: (k, 0, 0))
    fixed = pl.BlockSpec((ny, nx), lambda k: (0, 0))
    lane_block = pl.BlockSpec((ny, RING_COLS), lambda k: (0, 0))
    rows = pl.BlockSpec((1, 4, 2, nx), lambda k: (k, 0, 0, 0))
    out_shape = [jax.ShapeDtypeStruct((nz, ny, nx), jnp.float32)] * 4
    return pl.pallas_call(
        _step_kernel,
        grid=(nz,),
        in_specs=[fixed, lane_block, plane, plane, plane, plane, rows, rows, rows,
                  pl.BlockSpec((1, 4, RING_ROWS, RING_COLS), lambda k: (k, 0, 0, 0))],
        out_specs=[plane] * 4,
        out_shape=out_shape,
        scratch_shapes=[pltpu.VMEM((4, RING_ROWS, nx + RING_COLS), jnp.float32),
                        pltpu.VMEM((RING_ROWS, nx + RING_COLS), jnp.float32)],
        compiler_params=pltpu.CompilerParams(dimension_semantics=("arbitrary",)),
    )(levels, cor, *fields, north, fold, south, side)


def pack_side(west, east, sw, nw, se, ne):
    nc, nz, ny, _ = west.shape
    zero = jnp.zeros((nc, nz), jnp.float32)
    gap = jnp.zeros((nc, nz, RING_ROWS - ny - 2, 2), jnp.float32)

    def block(cols, top, bottom):
        return jnp.concatenate([cols, top[:, :, None, :], gap, bottom[:, :, None, :]], axis=2)

    east_block = block(east, jnp.stack([ne, zero], -1), jnp.stack([se, zero], -1))
    west_block = block(west, jnp.stack([zero, nw], -1), jnp.stack([zero, sw], -1))
    side = jnp.concatenate(
        [east_block, jnp.zeros((nc, nz, RING_ROWS, RING_COLS - 4), jnp.float32), west_block], axis=3)
    return jnp.swapaxes(side, 0, 1)


def flip_lanes_in_blocks(x):
    *lead, n = x.shape
    lane = jnp.arange(128)
    anti = lax.optimization_barrier((lane[:, None] + lane[None, :] == 127).astype(jnp.float32))
    flipped = jnp.einsum("...i,ij->...j", x.reshape(*lead, n // 128, 128), anti,
                         precision=lax.Precision.HIGHEST)
    return flipped.reshape(*lead, n)


def shift_pairs(count, step, wrap):
    pairs = []
    for i in range(count):
        j = i + step
        if wrap:
            pairs.append((i, j % count))
        elif 0 <= j < count:
            pairs.append((i, j))
    return pairs


def per_device(
    thermal_anomaly,
    saltiness_anomaly,
    zonal_velocity_array,
    meridional_velocity_array,
    seawater_profile_flags,
    submerged_layer_total,
    computed_block_flags,
):
    raw = (thermal_anomaly, saltiness_anomaly, zonal_velocity_array, meridional_velocity_array)
    block_depth_layers = thermal_anomaly.shape[0]
    block_meridional_extent = thermal_anomaly.shape[1]
    n_lon = lax.axis_size("lon")
    n_lat = lax.axis_size("lat")
    tile_alive = computed_block_flags[0, 0] == 1
    levels = jnp.where((seawater_profile_flags == 1) & tile_alive, submerged_layer_total, 0)
    depth_index = jnp.arange(block_depth_layers, dtype=jnp.int32)[:, None, None]

    def masked(rows, cols):
        wet = (depth_index < levels[None, rows, cols]).astype(jnp.float32)
        return jnp.stack([f[:, rows, cols] for f in raw]) * wet

    every = slice(None)
    last = n_lat - 1
    both = ("lon", "lat")
    nx = thermal_anomaly.shape[2]
    top = masked(slice(-2, None), every)
    folded = lax.ppermute(top, both, [(p * n_lat + last, (n_lon - 1 - p) * n_lat + last) for p in range(n_lon)])
    apart = lax.optimization_barrier(raw)
    wet_low = (depth_index < levels[None, 0:2, :]).astype(jnp.float32)
    bottom = jnp.stack([f[:, 0:2, :] for f in apart]) * wet_low
    from_south = lax.ppermute(top, "lat", shift_pairs(n_lat, 1, False))
    from_north = lax.ppermute(bottom, "lat", shift_pairs(n_lat, -1, False))
    signs = jnp.array([1.0, 1.0, -1.0, -1.0], jnp.float32).reshape(4, 1, 1, 1)
    is_northern = lax.axis_index("lat") == last

    def north_cols(cols):
        fold_part = jnp.stack(
            [jnp.stack([folded[:, :, 1 - r, nx - 1 - i] for i in cols], axis=-1) for r in range(2)], axis=2)
        return jnp.where(is_northern, fold_part * signs, from_north[..., cols[0]:cols[-1] + 1])

    def tall(cols):
        return jnp.concatenate(
            [from_south[..., cols[0]:cols[-1] + 1], masked(every, slice(cols[0], cols[-1] + 1)), north_cols(cols)],
            axis=2)

    west = lax.ppermute(tall((nx - 2, nx - 1)), "lon", shift_pairs(n_lon, 1, True))
    east = lax.ppermute(tall((0, 1)), "lon", shift_pairs(n_lon, -1, True))
    side = pack_side(west[:, :, 2:-2], east[:, :, 2:-2], west[:, :, 1, 1], west[:, :, -2, 1],
                     east[:, :, 1, 0], east[:, :, -2, 0])
    fold_rows = flip_lanes_in_blocks(folded) * signs
    total_rows = block_meridional_extent * n_lat
    row_pos = (
        lax.axis_index("lat") * block_meridional_extent
        + jnp.arange(block_meridional_extent, dtype=jnp.int32)
    ).astype(jnp.float32)
    coriolis = (CORIOLIS_MAX * jnp.sin(jnp.pi * ((row_pos + 0.5) / total_rows - 0.5)))[:, None]
    cor = jnp.broadcast_to(coriolis, (block_meridional_extent, RING_COLS))
    return tuple(stencil_call(levels, cor, raw, jnp.swapaxes(from_north, 0, 1), jnp.swapaxes(fold_rows, 0, 1),
                              jnp.swapaxes(from_south, 0, 1), side))


def solution(mesh):
    return jax.shard_map(
        per_device,
        mesh=mesh,
        in_specs=(
            P(None, "lat", "lon"),
            P(None, "lat", "lon"),
            P(None, "lat", "lon"),
            P(None, "lat", "lon"),
            P("lat", "lon"),
            P("lat", "lon"),
            P("lat", "lon"),
        ),
        out_specs=(
            P(None, "lat", "lon"),
            P(None, "lat", "lon"),
            P(None, "lat", "lon"),
            P(None, "lat", "lon"),
        ),
        check_vma=False,
    )
```
